32 devices in a mesh: seq: 16 (over z, y, core), mp: 2 (over x).
Axes of the slice: x: 2, y: 2, z: 4, core: 2. Of those that a mesh axis runs over, the one named last changes fastest.
Arguments:
- tokens: bfloat16 [4096, 2048], P('seq'), may hold values from -25 to 25
- lengths: int32 [32], replicated, may hold values from 1 to 1024, 4096 in all
- prefix_cache: bfloat16 [4, 2048, 512], P(None, 'seq'), may hold values from -1000 to 1000
- attn_gain: bfloat16 [2048], replicated, may hold values from 0.25 to 1.75
- w_query: bfloat16 [2048, 2048], P(None, 'mp'), may hold values from -0.25 to 0.25
- w_keyval: bfloat16 [2048, 512], replicated, may hold values from -0.125 to 0.125
- w_out: bfloat16 [2048, 2048], P('mp'), may hold values from -0.25 to 0.25
- final_gain: bfloat16 [2048], replicated, may hold values from 0.25 to 1.75
- w_head: bfloat16 [2048, 32000], P(None, ('seq', 'mp')), may hold values from -0.4375 to 0.4375
Outputs:
- hidden: bfloat16 [4096, 2048], P('seq', 'mp')
- suffix_cache: bfloat16 [4096, 512], P('seq')
- last_normed: bfloat16 [32, 2048], replicated
- greatest: float32 [32], replicated
The draws below stay inside these ranges and needn't reach their ends.
Inputs may be any that keep to these rules, and one draw needn't show every extreme that they name: The lengths sum to 4096 and one of them equals 1024.
All inputs are finite; a program needn't handle non-finite values.
Results may differ from the reference program's by a relative error of at most 0.013.
Values may be sent and summed in bfloat16 or wider, within the bound.
No kernel may reach another device: no remote copies, remote signals or barrier semaphores. Data moves between devices by JAX's collectives and lax.ppermute only.
A program may use at most 64 MiB of HBM per device.

```python
import math
import jax
import jax.numpy as jnp
import numpy as np
from jax import lax

D = 2048
QH = 32
KVH = 4
HD = 64
V = 32000
G = 4
RPG = 8
P_SIZE = 2048
MOST = 1024
TOK_DEV = 256
R = 32
TOKENS = 4096


def draw_tokens(key, part):
    first_key, second_key, third_key = jax.random.split(key, 3)
    base_draw = jnp.clip(jax.random.normal(first_key, (TOKENS, D), jnp.float32), -5.0, 5.0)
    column_scale = jnp.exp(jax.random.uniform(second_key, (1, D), jnp.float32, -1.15, 1.15))
    row_scale = jnp.exp(jax.random.uniform(third_key, (TOKENS, 1), jnp.float32, -1.15, 1.15))
    return (0.5 * base_draw * column_scale * row_scale).astype(jnp.bfloat16)


def draw_prefix_cache(key, part):
    first_key = jax.random.fold_in(key, 0)
    kv_width = KVH * HD
    base_draw = jnp.clip(jax.random.normal(first_key, (G, P_SIZE, 2 * kv_width), jnp.float32), -5.0, 5.0)
    return base_draw.astype(jnp.bfloat16)


def block_scale(rng, dims, cuts, least, top_value):
    factor_of, own = 1.0, jax.random.fold_in(rng, 6)
    for dim, shards_of in cuts:
        heights = jnp.exp(jax.random.uniform(jax.random.fold_in(own, dim), (shards_of,), jnp.float32, least / len(cuts), top_value / len(cuts)))
        factor_of = factor_of * jnp.repeat(heights, dims[dim] // shards_of).reshape([-1 if axis == dim else 1 for axis in range(len(dims))])
    return factor_of


def length_profile(count, total, reach, slope):
    loads = [(1 << 20) // math.isqrt(grade ** slope) + 1 for grade in range(2, count + 1)]
    spare, given = total - reach - (count - 1), [1] * (count - 1)
    while spare > 0:
        candidates = [i for i in range(count - 1) if given[i] < reach]
        pool, left = sum([loads[i] for i in candidates]), spare
        for i in candidates:
            more = min(reach - given[i], max(1, left * loads[i] // pool), spare)
            given[i] = given[i] + more
            spare = spare - more
    return np.array([reach] + given)


def ragged_sizes(stream_key, number_of, total, reach, lean):
    if number_of == 2:
        one = jax.random.randint(stream_key, (), max(1, total - reach), min(reach, total - 1) + 1)
        return jnp.stack([one, total - one])
    tallies = jnp.asarray(length_profile(number_of, total, reach, lean), jnp.int32)
    couples = (number_of - 1) // 2
    donor, sink = tallies[1:1 + 2 * couples:2], tallies[2:2 + 2 * couples:2]
    margin = jnp.minimum(donor - 1, reach - sink)
    shifted = jax.random.randint(jax.random.fold_in(stream_key, 1), (couples,), 0, 1 << 20) % (margin + 1)
    tallies = tallies.at[1:1 + 2 * couples:2].set(donor - shifted).at[2:2 + 2 * couples:2].set(sink + shifted)
    return tallies[jax.random.permutation(jax.random.fold_in(stream_key, 2), number_of)]


def bell_draw(key, extent, width, most, shards=(), kind=jnp.bfloat16):
    array = width * jax.random.normal(key, extent, jnp.float32)
    if shards:
        array = array * block_scale(key, extent, shards, -0.22, 0.18)
    return jnp.clip(array, -most, most).astype(kind)


def setup_inputs(seed: int = 0) -> dict:
    streams_of = jax.random.split(jax.random.key(seed), 10)
    tokens = draw_tokens(jax.random.fold_in(streams_of[9], 71), 0)
    lengths = ragged_sizes(streams_of[1], R, TOKENS, MOST, 2).astype(jnp.int32)
    prefix_cache = draw_prefix_cache(jax.random.fold_in(streams_of[9], 71), 0)
    attn_gain = jnp.clip(1.0 + 0.15 * jax.random.normal(streams_of[3], (D,), jnp.float32), 0.25, 1.75).astype(jnp.bfloat16)
    w_query = bell_draw(streams_of[4], (D, QH * HD), 0.044, 0.25, ((1, 2),))
    w_keyval = bell_draw(streams_of[5], (D, 2 * KVH * HD), D ** -0.5, 0.125)
    w_out = bell_draw(streams_of[6], (QH * HD, D), 0.044, 0.25, ((0, 2),))
    final_gain = jnp.clip(1.0 + 0.15 * jax.random.normal(streams_of[7], (D,), jnp.float32), 0.25, 1.75).astype(jnp.bfloat16)
    w_head = bell_draw(streams_of[8], (D, V), 0.07, 0.4375, ((1, 32),))
    return dict(tokens=tokens, lengths=lengths, prefix_cache=prefix_cache, attn_gain=attn_gain, w_query=w_query, w_keyval=w_keyval, w_out=w_out, final_gain=final_gain, w_head=w_head)


epsilon = 1e-05

def rotate(source, places, head_count):
    half_dim = HD // 2
    row_count = source.shape[0]
    reshaped = source.reshape(row_count, head_count, HD)
    frequency = 10000.0 ** (-(jnp.arange(half_dim, dtype=jnp.float32) * 2.0 / HD))
    angles = places.astype(jnp.float32)[:, None] * frequency[None, :]
    cos_table = jnp.cos(angles)[:, None, :]
    sine_table = jnp.sin(angles)[:, None, :]
    leading = reshaped[..., :half_dim]
    second = reshaped[..., half_dim:]
    joined = jnp.concatenate([leading * cos_table - second * sine_table, second * cos_table + leading * sine_table], -1)
    return joined.reshape(row_count, head_count * HD)

def reference(tokens, lengths, prefix_cache, attn_gain, w_query, w_keyval, w_out, final_gain, w_head):
    kv_width = KVH * HD
    group_size = QH // KVH
    activations = tokens.astype(jnp.float32)
    normed = (activations * lax.rsqrt(lax.optimization_barrier(jnp.mean(activations * activations, -1, keepdims=True)) + epsilon) * attn_gain.astype(jnp.float32)).astype(jnp.bfloat16)
    request_end = jnp.cumsum(lengths).astype(jnp.int32)
    starts = (request_end - lengths).astype(jnp.int32)
    position = jnp.arange(TOKENS, dtype=jnp.int32)
    request = lax.optimization_barrier(jnp.sum((position[:, None] >= request_end[None, :]).astype(jnp.int32), 1)).astype(jnp.int32)
    offset = (position - starts[request]).astype(jnp.int32)
    group_of = (request // RPG).astype(jnp.int32)
    query_full = jnp.dot(normed, w_query, preferred_element_type=jnp.float32)
    keyval = jnp.dot(normed, w_keyval, preferred_element_type=jnp.float32)
    queries = rotate(query_full, P_SIZE + offset, QH).astype(jnp.bfloat16)
    key_rows = rotate(keyval[:, :kv_width], P_SIZE + offset, KVH).astype(jnp.bfloat16)
    val_rows = keyval[:, kv_width:].astype(jnp.bfloat16)
    suffix_cache = jnp.concatenate([key_rows, val_rows], 1)
    all_keys = jnp.concatenate([prefix_cache[:, :, :kv_width].reshape(G * P_SIZE, kv_width), key_rows], 0).astype(jnp.float32).reshape(-1, KVH, HD)
    all_values = jnp.concatenate([prefix_cache[:, :, kv_width:].reshape(G * P_SIZE, kv_width), val_rows], 0).astype(jnp.float32).reshape(-1, KVH, HD)
    key_group = jnp.concatenate([jnp.repeat(jnp.arange(G, dtype=jnp.int32), P_SIZE), jnp.full((TOKENS,), -1, jnp.int32)])
    key_request = jnp.concatenate([jnp.full((G * P_SIZE,), -1, jnp.int32), request])
    key_place = jnp.concatenate([jnp.full((G * P_SIZE,), -1, jnp.int32), position])
    blocks = TOKENS // TOK_DEV

    def one_block(block_items):
        query_block, request_block, group_block, place_block = block_items
        allowed = (key_group[None, :] == group_block[:, None]) | (key_request[None, :] == request_block[:, None]) & (key_place[None, :] <= place_block[:, None])
        scores = jnp.einsum('bkgd,nkd->kgbn', query_block.astype(jnp.float32), all_keys) / math.sqrt(HD)
        scores = jnp.where(allowed[None, None], scores, -jnp.inf)
        row_max = lax.optimization_barrier(jnp.max(scores, -1, keepdims=True))
        weights = jnp.exp(scores - row_max)
        weight_sum = lax.optimization_barrier(jnp.sum(weights, -1))
        rounded = lax.optimization_barrier(weights.astype(jnp.bfloat16)).astype(jnp.float32)
        result = jnp.einsum('kgbn,nkd->bkgd', rounded, all_values) / jnp.transpose(weight_sum, (2, 0, 1))[..., None]
        return result.reshape(query_block.shape[0], QH * HD).astype(jnp.bfloat16)
    context = lax.map(one_block, (queries.reshape(blocks, TOK_DEV, KVH, group_size, HD), request.reshape(blocks, TOK_DEV), group_of.reshape(blocks, TOK_DEV), position.reshape(blocks, TOK_DEV)))
    context = context.reshape(TOKENS, QH * HD)
    hidden = (activations + jnp.dot(context, w_out, preferred_element_type=jnp.float32)).astype(jnp.bfloat16)
    last_rows = hidden[request_end - 1].astype(jnp.float32)
    inv_rms = lax.rsqrt(lax.optimization_barrier(jnp.mean(last_rows * last_rows, -1, keepdims=True)) + epsilon)
    last_normed = (last_rows * final_gain.astype(jnp.float32) * inv_rms).astype(jnp.bfloat16)
    logits = jnp.dot(last_normed, w_head, preferred_element_type=jnp.float32)
    greatest = lax.optimization_barrier(jnp.max(logits, -1))
    return (hidden, suffix_cache, last_normed, greatest)
```

```python
import math

import jax
import jax.numpy as jnp
from jax import lax
from jax.sharding import PartitionSpec as P

QH = 32
KVH = 4
HD = 64
G = 4
RPG = 8
P_SIZE = 2048
MOST = 1024
PREFIX_CHUNK = 512


epsilon = 1e-05


def rotate(source, places, head_count):
    half_dim = HD // 2
    row_count = source.shape[0]
    reshaped = source.reshape(row_count, head_count, HD)
    frequency = 10000.0 ** (-(jnp.arange(half_dim, dtype=jnp.float32) * 2.0 / HD))
    angles = places.astype(jnp.float32)[:, None] * frequency[None, :]
    cos_table = jnp.cos(angles)[:, None, :]
    sine_table = jnp.sin(angles)[:, None, :]
    leading = reshaped[..., :half_dim]
    second = reshaped[..., half_dim:]
    joined = jnp.concatenate(
        [leading * cos_table - second * sine_table, second * cos_table + leading * sine_table], -1
    )
    return joined.reshape(row_count, head_count * HD)


def attend(running, queries, kv_block, allowed):
    old_max, old_sum, numerator = running
    half_width = kv_block.shape[1] // 2
    kv_heads = queries.shape[1]
    key_rows = kv_block[:, :half_width].reshape(kv_block.shape[0], kv_heads, HD)
    val_rows = kv_block[:, half_width:].reshape(kv_block.shape[0], kv_heads, HD)
    scores = jnp.einsum("qgrd,ngd->grqn", queries, key_rows, preferred_element_type=jnp.float32) * (
        1.0 / math.sqrt(HD)
    )
    scores = jnp.where(allowed[None, None], scores, -jnp.inf)
    new_max = jnp.maximum(old_max, jnp.max(scores, -1))
    factor = jnp.exp(old_max - new_max)
    weights = jnp.exp(scores - new_max[..., None])
    new_sum = old_sum * factor + jnp.sum(weights, -1)
    numerator = numerator * factor[..., None] + jnp.einsum(
        "grqn,ngd->grqd", weights.astype(jnp.bfloat16), val_rows, preferred_element_type=jnp.float32
    )
    return (new_max, new_sum, numerator)


def shifted_back(block, axis, distance):
    count = lax.axis_size(axis)
    route = [(i, i + distance) for i in range(count - distance)]
    return lax.ppermute(block, axis, route)


def per_device(
    tokens, lengths, prefix_cache, attn_gain, w_query, w_keyval, w_out, final_gain, w_head
):
    token_rows = tokens.shape[0]
    model_width = tokens.shape[1]
    seq_devices = lax.axis_size("seq")
    seq_index = lax.axis_index("seq")
    mp_index = lax.axis_index("mp")
    part_width = model_width // lax.axis_size("mp")
    query_heads = w_query.shape[1] // HD
    group_size = QH // KVH
    kv_heads = max(1, query_heads // group_size)
    repeat_count = query_heads // kv_heads
    kv_first = mp_index * query_heads // group_size
    kv_width = KVH * HD
    request_count = lengths.shape[0]
    back_blocks = min(seq_devices - 1, -(-(MOST - 1) // token_rows))

    own_prefix = jnp.concatenate(
        [
            lax.dynamic_slice_in_dim(prefix_cache, kv_first * HD, kv_heads * HD, 2),
            lax.dynamic_slice_in_dim(prefix_cache, kv_width + kv_first * HD, kv_heads * HD, 2),
        ],
        2,
    )
    prefix_rows = own_prefix.shape[1]
    block_width = own_prefix.shape[2]
    all_prefix = lax.all_gather(own_prefix, "seq", axis=0)

    activations = tokens.astype(jnp.float32)
    normed = (
        activations
        * lax.rsqrt(jnp.mean(activations * activations, -1, keepdims=True) + epsilon)
        * attn_gain.astype(jnp.float32)
    ).astype(jnp.bfloat16)
    request_end = jnp.cumsum(lengths)
    starts = request_end - lengths
    position = seq_index * token_rows + jnp.arange(token_rows, dtype=jnp.int32)
    request = jnp.sum((position[:, None] >= request_end[None, :]).astype(jnp.int32), 1)
    request_table = request[:, None] == jnp.arange(request_count, dtype=jnp.int32)[None, :]
    offset = position - jnp.sum(jnp.where(request_table, starts[None, :], 0), 1)
    group_of = request // RPG
    keyval = jnp.dot(normed, w_keyval, preferred_element_type=jnp.float32)
    key_rows = rotate(keyval[:, :kv_width], P_SIZE + offset, KVH).astype(jnp.bfloat16)
    val_rows = keyval[:, kv_width:].astype(jnp.bfloat16)
    suffix_cache = jnp.concatenate([key_rows, val_rows], 1)
    own_suffix = jnp.concatenate(
        [
            lax.dynamic_slice_in_dim(key_rows, kv_first * HD, kv_heads * HD, 1),
            lax.dynamic_slice_in_dim(val_rows, kv_first * HD, kv_heads * HD, 1),
        ],
        1,
    )
    earlier = [own_suffix] + [
        shifted_back(own_suffix, "seq", distance) for distance in range(1, back_blocks + 1)
    ]
    suffix_window = jnp.stack(earlier, 0)

    query_full = jnp.dot(normed, w_query, preferred_element_type=jnp.float32)
    queries = (
        rotate(query_full, P_SIZE + offset, query_heads)
        .astype(jnp.bfloat16)
        .reshape(token_rows, kv_heads, repeat_count, HD)
    )

    running = (
        jnp.full((kv_heads, repeat_count, token_rows), -1e30, jnp.float32),
        jnp.zeros((kv_heads, repeat_count, token_rows), jnp.float32),
        jnp.zeros((kv_heads, repeat_count, token_rows, HD), jnp.float32),
    )

    sources_per_chunk = max(1, PREFIX_CHUNK // prefix_rows)
    chunks_per_group = seq_devices // sources_per_chunk
    first_group = group_of[0]
    last_group = group_of[token_rows - 1]

    def prefix_step(chunk, state_now):
        group = chunk // chunks_per_group
        part = chunk % chunks_per_group
        block = lax.dynamic_slice(
            all_prefix,
            (part * sources_per_chunk, group, 0, 0),
            (sources_per_chunk, 1, prefix_rows, block_width),
        ).reshape(sources_per_chunk * prefix_rows, block_width)
        allowed = jnp.broadcast_to(
            (group_of == group)[:, None], (token_rows, sources_per_chunk * prefix_rows)
        )
        return attend(state_now, queries, block, allowed)

    running = lax.fori_loop(
        first_group * chunks_per_group, (last_group + 1) * chunks_per_group, prefix_step, running
    )

    first_block = starts[request[0]] // token_rows
    back_needed = jnp.minimum(seq_index - first_block, back_blocks)

    def suffix_step(distance, state_now):
        source_dev = seq_index - distance
        key_place = source_dev * token_rows + jnp.arange(token_rows, dtype=jnp.int32)
        key_request = jnp.sum((key_place[:, None] >= request_end[None, :]).astype(jnp.int32), 1)
        allowed = (
            (request[:, None] == key_request[None, :])
            & (key_place[None, :] <= position[:, None])
            & (source_dev >= 0)
        )
        block = lax.dynamic_index_in_dim(suffix_window, distance, 0, keepdims=False)
        return attend(state_now, queries, block, allowed)

    running = lax.fori_loop(0, back_needed + 1, suffix_step, running)

    final_max, final_sum, numerator = running
    context = numerator / final_sum[..., None]
    context = (
        jnp.transpose(context, (2, 0, 1, 3))
        .reshape(token_rows, query_heads * HD)
        .astype(jnp.bfloat16)
    )
    mixture = jnp.dot(context, w_out, preferred_element_type=jnp.float32)
    mixture = lax.psum_scatter(
        mixture.astype(jnp.bfloat16), "mp", scatter_dimension=1, tiled=True
    ).astype(jnp.float32)
    own_columns = lax.dynamic_slice_in_dim(activations, mp_index * part_width, part_width, 1)
    hidden = (own_columns + mixture).astype(jnp.bfloat16)
    local_last = request_end - 1 - seq_index * token_rows
    onehot = (local_last[:, None] == jnp.arange(token_rows, dtype=jnp.int32)[None, :]).astype(
        jnp.bfloat16
    )
    last_part = jnp.dot(onehot, hidden, preferred_element_type=jnp.float32).astype(jnp.bfloat16)
    last_part = lax.psum(last_part, "seq")
    last_rows = lax.all_gather(last_part, "mp", axis=1, tiled=True).astype(jnp.float32)
    inv_rms = lax.rsqrt(jnp.mean(last_rows * last_rows, -1, keepdims=True) + epsilon)
    last_normed = (last_rows * final_gain.astype(jnp.float32) * inv_rms).astype(jnp.bfloat16)
    logits = jnp.dot(last_normed, w_head, preferred_element_type=jnp.float32)
    greatest = lax.pmax(jnp.max(logits, -1), ("seq", "mp"))
    return (hidden, suffix_cache, last_normed, greatest)


def solution(mesh):
    return jax.shard_map(
        per_device,
        mesh=mesh,
        in_specs=(
            P("seq", None),
            P(),
            P(None, "seq", None),
            P(),
            P(None, "mp"),
            P(),
            P("mp", None),
            P(),
            P(None, ("seq", "mp")),
        ),
        out_specs=(P("seq", "mp"), P("seq", None), P(), P()),
        check_vma=False,
    )
```

```python
import math

import jax
import jax.numpy as jnp
from jax import lax
from jax.sharding import PartitionSpec as P

QH = 32
KVH = 4
HD = 64
G = 4
RPG = 8
P_SIZE = 2048
MOST = 1024
PREFIX_CHUNK = 512


epsilon = 1e-05


def rotate(source, places, head_count):
    half_dim = HD // 2
    row_count = source.shape[0]
    reshaped = source.reshape(row_count, head_count, HD)
    frequency = 10000.0 ** (-(jnp.arange(half_dim, dtype=jnp.float32) * 2.0 / HD))
    angles = places.astype(jnp.float32)[:, None] * frequency[None, :]
    cos_table = jnp.cos(angles)[:, None, :]
    sine_table = jnp.sin(angles)[:, None, :]
    leading = reshaped[..., :half_dim]
    second = reshaped[..., half_dim:]
    joined = jnp.concatenate(
        [leading * cos_table - second * sine_table, second * cos_table + leading * sine_table], -1
    )
    return joined.reshape(row_count, head_count * HD)


def attend(running, queries, kv_block, allowed):
    old_max, old_sum, numerator = running
    half_width = kv_block.shape[1] // 2
    kv_heads = queries.shape[1]
    key_rows = kv_block[:, :half_width].reshape(kv_block.shape[0], kv_heads, HD)
    val_rows = kv_block[:, half_width:].reshape(kv_block.shape[0], kv_heads, HD)
    scores = jnp.einsum("qgrd,ngd->grqn", queries, key_rows, preferred_element_type=jnp.float32) * (
        1.0 / math.sqrt(HD)
    )
    scores = jnp.where(allowed[None, None], scores, -jnp.inf)
    new_max = jnp.maximum(old_max, jnp.max(scores, -1))
    factor = jnp.exp(old_max - new_max)
    weights = jnp.exp(scores - new_max[..., None])
    new_sum = old_sum * factor + jnp.sum(weights, -1)
    numerator = numerator * factor[..., None] + jnp.einsum(
        "grqn,ngd->grqd", weights.astype(jnp.bfloat16), val_rows, preferred_element_type=jnp.float32
    )
    return (new_max, new_sum, numerator)


def butterfly(block, axis, combine):
    count = lax.axis_size(axis)
    if count & (count - 1):
        return None
    step = 1
    while step < count:
        partner = lax.ppermute(block, axis, [(i, i ^ step) for i in range(count)])
        block = combine(block, partner)
        step *= 2
    return block


def shifted_back(block, axis, distance):
    count = lax.axis_size(axis)
    route = [(i, i + distance) for i in range(count - distance)]
    return lax.ppermute(block, axis, route)


def per_device(
    tokens, lengths, prefix_cache, attn_gain, w_query, w_keyval, w_out, final_gain, w_head
):
    token_rows = tokens.shape[0]
    model_width = tokens.shape[1]
    seq_devices = lax.axis_size("seq")
    seq_index = lax.axis_index("seq")
    mp_index = lax.axis_index("mp")
    part_width = model_width // lax.axis_size("mp")
    query_heads = w_query.shape[1] // HD
    group_size = QH // KVH
    kv_heads = max(1, query_heads // group_size)
    repeat_count = query_heads // kv_heads
    kv_first = mp_index * query_heads // group_size
    kv_width = KVH * HD
    request_count = lengths.shape[0]
    back_blocks = min(seq_devices - 1, -(-(MOST - 1) // token_rows))

    own_prefix = jnp.concatenate(
        [
            lax.dynamic_slice_in_dim(prefix_cache, kv_first * HD, kv_heads * HD, 2),
            lax.dynamic_slice_in_dim(prefix_cache, kv_width + kv_first * HD, kv_heads * HD, 2),
        ],
        2,
    )
    prefix_rows = own_prefix.shape[1]
    block_width = own_prefix.shape[2]
    all_prefix = lax.all_gather(own_prefix, "seq", axis=0)

    activations = tokens.astype(jnp.float32)
    normed = (
        activations
        * lax.rsqrt(jnp.mean(activations * activations, -1, keepdims=True) + epsilon)
        * attn_gain.astype(jnp.float32)
    ).astype(jnp.bfloat16)
    request_end = jnp.cumsum(lengths)
    starts = request_end - lengths
    position = seq_index * token_rows + jnp.arange(token_rows, dtype=jnp.int32)
    request = jnp.sum((position[:, None] >= request_end[None, :]).astype(jnp.int32), 1)
    request_table = request[:, None] == jnp.arange(request_count, dtype=jnp.int32)[None, :]
    offset = position - jnp.sum(jnp.where(request_table, starts[None, :], 0), 1)
    group_of = request // RPG
    keyval = jnp.dot(normed, w_keyval, preferred_element_type=jnp.float32)
    key_rows = rotate(keyval[:, :kv_width], P_SIZE + offset, KVH).astype(jnp.bfloat16)
    val_rows = keyval[:, kv_width:].astype(jnp.bfloat16)
    suffix_cache = jnp.concatenate([key_rows, val_rows], 1)
    own_suffix = jnp.concatenate(
        [
            lax.dynamic_slice_in_dim(key_rows, kv_first * HD, kv_heads * HD, 1),
            lax.dynamic_slice_in_dim(val_rows, kv_first * HD, kv_heads * HD, 1),
        ],
        1,
    )
    earlier = [own_suffix] + [
        shifted_back(own_suffix, "seq", distance) for distance in range(1, back_blocks + 1)
    ]
    suffix_window = jnp.stack(earlier, 0)

    query_full = jnp.dot(normed, w_query, preferred_element_type=jnp.float32)
    queries = (
        rotate(query_full, P_SIZE + offset, query_heads)
        .astype(jnp.bfloat16)
        .reshape(token_rows, kv_heads, repeat_count, HD)
    )

    running = (
        jnp.full((kv_heads, repeat_count, token_rows), -1e30, jnp.float32),
        jnp.zeros((kv_heads, repeat_count, token_rows), jnp.float32),
        jnp.zeros((kv_heads, repeat_count, token_rows, HD), jnp.float32),
    )

    sources_per_chunk = max(1, PREFIX_CHUNK // prefix_rows)
    chunks_per_group = seq_devices // sources_per_chunk
    first_group = group_of[0]
    last_group = group_of[token_rows - 1]

    def prefix_step(chunk, state_now):
        group = chunk // chunks_per_group
        part = chunk % chunks_per_group
        block = lax.dynamic_slice(
            all_prefix,
            (part * sources_per_chunk, group, 0, 0),
            (sources_per_chunk, 1, prefix_rows, block_width),
        ).reshape(sources_per_chunk * prefix_rows, block_width)
        allowed = jnp.broadcast_to(
            (group_of == group)[:, None], (token_rows, sources_per_chunk * prefix_rows)
        )
        return attend(state_now, queries, block, allowed)

    running = lax.fori_loop(
        first_group * chunks_per_group, (last_group + 1) * chunks_per_group, prefix_step, running
    )

    first_block = starts[request[0]] // token_rows
    back_needed = jnp.minimum(seq_index - first_block, back_blocks)

    def suffix_step(distance, state_now):
        source_dev = seq_index - distance
        key_place = source_dev * token_rows + jnp.arange(token_rows, dtype=jnp.int32)
        key_request = jnp.sum((key_place[:, None] >= request_end[None, :]).astype(jnp.int32), 1)
        allowed = (
            (request[:, None] == key_request[None, :])
            & (key_place[None, :] <= position[:, None])
            & (source_dev >= 0)
        )
        block = lax.dynamic_index_in_dim(suffix_window, distance, 0, keepdims=False)
        return attend(state_now, queries, block, allowed)

    running = lax.fori_loop(0, back_needed + 1, suffix_step, running)

    final_max, final_sum, numerator = running
    context = numerator / final_sum[..., None]
    context = (
        jnp.transpose(context, (2, 0, 1, 3))
        .reshape(token_rows, query_heads * HD)
        .astype(jnp.bfloat16)
    )
    mixture = jnp.dot(context, w_out, preferred_element_type=jnp.float32)
    mp_devices = lax.axis_size("mp")
    own_columns = lax.dynamic_slice_in_dim(activations, mp_index * part_width, part_width, 1)
    if mp_devices == 2:
        kept = lax.dynamic_slice_in_dim(mixture, mp_index * part_width, part_width, 1)
        sent = lax.dynamic_slice_in_dim(mixture, (1 - mp_index) * part_width, part_width, 1)
        received = lax.ppermute(sent.astype(jnp.bfloat16), "mp", [(0, 1), (1, 0)])
        hidden = (own_columns + (kept + received.astype(jnp.float32))).astype(jnp.bfloat16)
    else:
        mixture = lax.psum_scatter(
            mixture.astype(jnp.bfloat16), "mp", scatter_dimension=1, tiled=True
        ).astype(jnp.float32)
        hidden = (own_columns + mixture).astype(jnp.bfloat16)
    local_last = request_end - 1 - seq_index * token_rows
    onehot = (local_last[:, None] == jnp.arange(token_rows, dtype=jnp.int32)[None, :]).astype(
        jnp.bfloat16
    )
    last_part = jnp.dot(onehot, hidden, preferred_element_type=jnp.float32).astype(jnp.bfloat16)
    summed = butterfly(last_part, "seq", jnp.add)
    if summed is None:
        summed = lax.psum(last_part, "seq")
    last_rows = lax.all_gather(summed, "mp", axis=1, tiled=True).astype(jnp.float32)
    inv_rms = lax.rsqrt(jnp.mean(last_rows * last_rows, -1, keepdims=True) + epsilon)
    last_normed = (last_rows * final_gain.astype(jnp.float32) * inv_rms).astype(jnp.bfloat16)
    logits = jnp.dot(last_normed, w_head, preferred_element_type=jnp.float32)
    local_best = jnp.max(logits, -1)
    best_seq = butterfly(local_best, "seq", jnp.maximum)
    best_all = None if best_seq is None else butterfly(best_seq, "mp", jnp.maximum)
    greatest = lax.pmax(local_best, ("seq", "mp")) if best_all is None else best_all
    return (hidden, suffix_cache, last_normed, greatest)


def solution(mesh):
    return jax.shard_map(
        per_device,
        mesh=mesh,
        in_specs=(
            P("seq", None),
            P(),
            P(None, "seq", None),
            P(),
            P(None, "mp"),
            P(),
            P("mp", None),
            P(),
            P(None, ("seq", "mp")),
        ),
        out_specs=(P("seq", "mp"), P("seq", None), P(), P()),
        check_vma=False,
    )
```

```python
import functools
import math

import jax
import jax.numpy as jnp
from jax import lax
from jax.experimental import pallas as pl
from jax.experimental.pallas import tpu as pltpu
from jax.sharding import PartitionSpec as P

QH = 32
KVH = 4
HD = 64
G = 4
RPG = 8
P_SIZE = 2048
MOST = 1024
PREFIX_CHUNK = 512
SUFFIX_CHUNK = 256
TILE_TOKENS = 128


epsilon = 1e-05


def rotate(source, places, head_count):
    half_dim = HD // 2
    row_count = source.shape[0]
    reshaped = source.reshape(row_count, head_count, HD)
    frequency = 10000.0 ** (-(jnp.arange(half_dim, dtype=jnp.float32) * 2.0 / HD))
    angles = places.astype(jnp.float32)[:, None] * frequency[None, :]
    cos_table = jnp.cos(angles)[:, None, :]
    sine_table = jnp.sin(angles)[:, None, :]
    leading = reshaped[..., :half_dim]
    second = reshaped[..., half_dim:]
    joined = jnp.concatenate(
        [leading * cos_table - second * sine_table, second * cos_table + leading * sine_table], -1
    )
    return joined.reshape(row_count, head_count * HD)


def attend(running, queries, kv_block, allowed):
    old_max, old_sum, numerator = running
    half_width = kv_block.shape[1] // 2
    kv_heads = queries.shape[1]
    key_rows = kv_block[:, :half_width].reshape(kv_block.shape[0], kv_heads, HD)
    val_rows = kv_block[:, half_width:].reshape(kv_block.shape[0], kv_heads, HD)
    scores = jnp.einsum("qgrd,ngd->grqn", queries, key_rows, preferred_element_type=jnp.float32) * (
        1.0 / math.sqrt(HD)
    )
    scores = jnp.where(allowed[None, None], scores, -jnp.inf)
    new_max = jnp.maximum(old_max, jnp.max(scores, -1))
    factor = jnp.exp(old_max - new_max)
    weights = jnp.exp(scores - new_max[..., None])
    new_sum = old_sum * factor + jnp.sum(weights, -1)
    numerator = numerator * factor[..., None] + jnp.einsum(
        "grqn,ngd->grqd", weights.astype(jnp.bfloat16), val_rows, preferred_element_type=jnp.float32
    )
    return (new_max, new_sum, numerator)


def attention_kernel(
    table, q_ref, rg_ref, rr_ref, rp_ref, pk_ref, pv_ref, sk_ref, sv_ref, kr_ref, kp_ref,
    o_ref, m_ref, l_ref, acc_ref, *, kv_heads, prefix_chunk, suffix_chunk, chunks_per_group
):
    tile = pl.program_id(0)
    p_lo = table[4 * tile]
    p_hi = table[4 * tile + 1]
    s_lo = table[4 * tile + 2]
    s_hi = table[4 * tile + 3]
    row_group = rg_ref[...]
    row_request = rr_ref[...]
    row_place = rp_ref[...]
    for head in range(kv_heads):
        query = q_ref[head]
        m_ref[...] = jnp.full(m_ref.shape, -1e30, jnp.float32)
        l_ref[...] = jnp.zeros(l_ref.shape, jnp.float32)
        acc_ref[...] = jnp.zeros(acc_ref.shape, jnp.float32)

        def update(key, value, allowed):
            scores = lax.dot_general(
                query, key, (((1,), (1,)), ((), ())), preferred_element_type=jnp.float32
            ) * (1.0 / math.sqrt(HD))
            scores = jnp.where(allowed, scores, -jnp.inf)
            old_max = m_ref[...]
            new_max = jnp.maximum(old_max, jnp.max(scores, axis=1, keepdims=True))
            factor = jnp.exp(old_max - new_max)
            weights = jnp.exp(scores - new_max)
            l_ref[...] = l_ref[...] * factor + jnp.sum(weights, axis=1, keepdims=True)
            acc_ref[...] = acc_ref[...] * factor + jnp.dot(
                weights.astype(jnp.bfloat16), value, preferred_element_type=jnp.float32
            )
            m_ref[...] = new_max

        def prefix_step(chunk, carry):
            start = pl.multiple_of(chunk * prefix_chunk, prefix_chunk)
            key = pk_ref[head, pl.ds(start, prefix_chunk), :]
            value = pv_ref[head, pl.ds(start, prefix_chunk), :]
            update(key, value, row_group == chunk // chunks_per_group)
            return carry

        lax.fori_loop(p_lo, p_hi, prefix_step, 0)

        def suffix_step(chunk, carry):
            start = pl.multiple_of(chunk * suffix_chunk, suffix_chunk)
            key = sk_ref[head, pl.ds(start, suffix_chunk), :]
            value = sv_ref[head, pl.ds(start, suffix_chunk), :]
            key_request = kr_ref[pl.ds(chunk, 1), :]
            key_place = kp_ref[pl.ds(chunk, 1), :]
            update(key, value, (row_request == key_request) & (key_place <= row_place))
            return carry

        lax.fori_loop(s_lo, s_hi, suffix_step, 0)
        o_ref[head] = (acc_ref[...] / l_ref[...]).astype(o_ref.dtype)


def butterfly(block, axis, combine):
    count = lax.axis_size(axis)
    if count & (count - 1):
        return None
    step = 1
    while step < count:
        partner = lax.ppermute(block, axis, [(i, i ^ step) for i in range(count)])
        block = combine(block, partner)
        step *= 2
    return block


def shifted_back(block, axis, distance):
    count = lax.axis_size(axis)
    route = [(i, i + distance) for i in range(count - distance)]
    return lax.ppermute(block, axis, route)


def per_device(
    tokens, lengths, prefix_cache, attn_gain, w_query, w_keyval, w_out, final_gain, w_head
):
    token_rows = tokens.shape[0]
    model_width = tokens.shape[1]
    seq_devices = lax.axis_size("seq")
    seq_index = lax.axis_index("seq")
    mp_index = lax.axis_index("mp")
    part_width = model_width // lax.axis_size("mp")
    query_heads = w_query.shape[1] // HD
    group_size = QH // KVH
    kv_heads = max(1, query_heads // group_size)
    repeat_count = query_heads // kv_heads
    kv_first = mp_index * query_heads // group_size
    kv_width = KVH * HD
    request_count = lengths.shape[0]
    back_blocks = min(seq_devices - 1, -(-(MOST - 1) // token_rows))

    own_prefix = jnp.concatenate(
        [
            lax.dynamic_slice_in_dim(prefix_cache, kv_first * HD, kv_heads * HD, 2),
            lax.dynamic_slice_in_dim(prefix_cache, kv_width + kv_first * HD, kv_heads * HD, 2),
        ],
        2,
    )
    prefix_rows = own_prefix.shape[1]
    block_width = own_prefix.shape[2]
    all_prefix = lax.all_gather(own_prefix, "seq", axis=0)

    activations = tokens.astype(jnp.float32)
    normed = (
        activations
        * lax.rsqrt(jnp.mean(activations * activations, -1, keepdims=True) + epsilon)
        * attn_gain.astype(jnp.float32)
    ).astype(jnp.bfloat16)
    request_end = jnp.cumsum(lengths)
    starts = request_end - lengths
    position = seq_index * token_rows + jnp.arange(token_rows, dtype=jnp.int32)
    request = jnp.sum((position[:, None] >= request_end[None, :]).astype(jnp.int32), 1)
    request_table = request[:, None] == jnp.arange(request_count, dtype=jnp.int32)[None, :]
    offset = position - jnp.sum(jnp.where(request_table, starts[None, :], 0), 1)
    group_of = request // RPG
    keyval = jnp.dot(normed, w_keyval, preferred_element_type=jnp.float32)
    key_rows = rotate(keyval[:, :kv_width], P_SIZE + offset, KVH).astype(jnp.bfloat16)
    val_rows = keyval[:, kv_width:].astype(jnp.bfloat16)
    suffix_cache = jnp.concatenate([key_rows, val_rows], 1)
    own_suffix = jnp.concatenate(
        [
            lax.dynamic_slice_in_dim(key_rows, kv_first * HD, kv_heads * HD, 1),
            lax.dynamic_slice_in_dim(val_rows, kv_first * HD, kv_heads * HD, 1),
        ],
        1,
    )
    earlier = [own_suffix] + [
        shifted_back(own_suffix, "seq", distance) for distance in range(1, back_blocks + 1)
    ]

    query_full = jnp.dot(normed, w_query, preferred_element_type=jnp.float32)
    queries = (
        rotate(query_full, P_SIZE + offset, query_heads)
        .astype(jnp.bfloat16)
        .reshape(token_rows, kv_heads, repeat_count, HD)
    )

    window_blocks = back_blocks + 1
    window_rows = window_blocks * token_rows
    window_start = (seq_index - back_blocks) * token_rows
    suffix_window = jnp.concatenate(earlier[::-1], 0)
    suffix_keys = jnp.transpose(
        suffix_window[:, : kv_heads * HD].reshape(window_rows, kv_heads, HD), (1, 0, 2)
    )
    suffix_values = jnp.transpose(
        suffix_window[:, kv_heads * HD :].reshape(window_rows, kv_heads, HD), (1, 0, 2)
    )
    prefix_total = seq_devices * prefix_rows
    prefix_flat = jnp.transpose(all_prefix, (1, 0, 2, 3)).reshape(G * prefix_total, block_width)
    prefix_keys = jnp.transpose(
        prefix_flat[:, : kv_heads * HD].reshape(G * prefix_total, kv_heads, HD), (1, 0, 2)
    )
    prefix_values = jnp.transpose(
        prefix_flat[:, kv_heads * HD :].reshape(G * prefix_total, kv_heads, HD), (1, 0, 2)
    )
    suffix_chunk = min(SUFFIX_CHUNK, token_rows)
    prefix_chunk = min(PREFIX_CHUNK, prefix_total)
    chunks_per_group = prefix_total // prefix_chunk
    suffix_chunks = window_rows // suffix_chunk
    key_place = window_start + jnp.arange(window_rows, dtype=jnp.int32)
    key_request = jnp.sum((key_place[:, None] >= request_end[None, :]).astype(jnp.int32), 1)
    key_request = jnp.where(key_place >= 0, key_request, -1)
    key_request = key_request.reshape(suffix_chunks, suffix_chunk)
    key_place = key_place.reshape(suffix_chunks, suffix_chunk)

    tile_tokens = min(TILE_TOKENS, token_rows)
    tile_count = token_rows // tile_tokens
    tile_rows = tile_tokens * repeat_count
    first_token = jnp.arange(tile_count, dtype=jnp.int32) * tile_tokens
    last_token = first_token + tile_tokens - 1
    p_lo = group_of[first_token] * chunks_per_group
    p_hi = (group_of[last_token] + 1) * chunks_per_group
    s_lo = jnp.maximum((starts[request[first_token]] - window_start) // suffix_chunk, 0)
    s_hi = jnp.minimum((position[last_token] - window_start) // suffix_chunk + 1, suffix_chunks)
    table = jnp.stack([p_lo, p_hi, s_lo, s_hi], 1).reshape(-1).astype(jnp.int32)

    query_rows = jnp.transpose(queries, (1, 0, 2, 3)).reshape(
        kv_heads, token_rows * repeat_count, HD
    )
    row_group = jnp.repeat(group_of, repeat_count)[:, None]
    row_request = jnp.repeat(request, repeat_count)[:, None]
    row_place = jnp.repeat(position, repeat_count)[:, None]

    def whole(shape):
        return pl.BlockSpec(shape, lambda tile, table: (0,) * len(shape))

    row_spec = pl.BlockSpec((tile_rows, 1), lambda tile, table: (tile, 0))
    context = pl.pallas_call(
        functools.partial(
            attention_kernel,
            kv_heads=kv_heads,
            prefix_chunk=prefix_chunk,
            suffix_chunk=suffix_chunk,
            chunks_per_group=chunks_per_group,
        ),
        grid_spec=pltpu.PrefetchScalarGridSpec(
            num_scalar_prefetch=1,
            grid=(tile_count,),
            in_specs=[
                pl.BlockSpec((kv_heads, tile_rows, HD), lambda tile, table: (0, tile, 0)),
                row_spec,
                row_spec,
                row_spec,
                whole(prefix_keys.shape),
                whole(prefix_values.shape),
                whole(suffix_keys.shape),
                whole(suffix_values.shape),
                whole(key_request.shape),
                whole(key_place.shape),
            ],
            out_specs=pl.BlockSpec((kv_heads, tile_rows, HD), lambda tile, table: (0, tile, 0)),
            scratch_shapes=[
                pltpu.VMEM((tile_rows, 1), jnp.float32),
                pltpu.VMEM((tile_rows, 1), jnp.float32),
                pltpu.VMEM((tile_rows, HD), jnp.float32),
            ],
        ),
        out_shape=jax.ShapeDtypeStruct((kv_heads, token_rows * repeat_count, HD), jnp.bfloat16),
    )(
        table, query_rows, row_group, row_request, row_place, prefix_keys, prefix_values,
        suffix_keys, suffix_values, key_request, key_place,
    )
    context = jnp.transpose(
        context.reshape(kv_heads, token_rows, repeat_count, HD), (1, 0, 2, 3)
    ).reshape(token_rows, query_heads * HD)
    mixture = jnp.dot(context, w_out, preferred_element_type=jnp.float32)
    mp_devices = lax.axis_size("mp")
    own_columns = lax.dynamic_slice_in_dim(activations, mp_index * part_width, part_width, 1)
    if mp_devices == 2:
        kept = lax.dynamic_slice_in_dim(mixture, mp_index * part_width, part_width, 1)
        sent = lax.dynamic_slice_in_dim(mixture, (1 - mp_index) * part_width, part_width, 1)
        received = lax.ppermute(sent.astype(jnp.bfloat16), "mp", [(0, 1), (1, 0)])
        hidden = (own_columns + (kept + received.astype(jnp.float32))).astype(jnp.bfloat16)
    else:
        mixture = lax.psum_scatter(
            mixture.astype(jnp.bfloat16), "mp", scatter_dimension=1, tiled=True
        ).astype(jnp.float32)
        hidden = (own_columns + mixture).astype(jnp.bfloat16)
    local_last = request_end - 1 - seq_index * token_rows
    onehot = (local_last[:, None] == jnp.arange(token_rows, dtype=jnp.int32)[None, :]).astype(
        jnp.bfloat16
    )
    last_part = jnp.dot(onehot, hidden, preferred_element_type=jnp.float32).astype(jnp.bfloat16)
    summed = butterfly(last_part, "seq", jnp.add)
    if summed is None:
        summed = lax.psum(last_part, "seq")
    last_rows = lax.all_gather(summed, "mp", axis=1, tiled=True).astype(jnp.float32)
    inv_rms = lax.rsqrt(jnp.mean(last_rows * last_rows, -1, keepdims=True) + epsilon)
    last_normed = (last_rows * final_gain.astype(jnp.float32) * inv_rms).astype(jnp.bfloat16)
    logits = jnp.dot(last_normed, w_head, preferred_element_type=jnp.float32)
    local_best = jnp.max(logits, -1)
    best_seq = butterfly(local_best, "seq", jnp.maximum)
    best_all = None if best_seq is None else butterfly(best_seq, "mp", jnp.maximum)
    greatest = lax.pmax(local_best, ("seq", "mp")) if best_all is None else best_all
    return (hidden, suffix_cache, last_normed, greatest)


def solution(mesh):
    return jax.shard_map(
        per_device,
        mesh=mesh,
        in_specs=(
            P("seq", None),
            P(),
            P(None, "seq", None),
            P(),
            P(None, "mp"),
            P(),
            P("mp", None),
            P(),
            P(None, ("seq", "mp")),
        ),
        out_specs=(P("seq", "mp"), P("seq", None), P(), P()),
        check_vma=False,
    )
```

```python
import functools
import math

import jax
import jax.numpy as jnp
from jax import lax
from jax.experimental import pallas as pl
from jax.experimental.pallas import tpu as pltpu
from jax.sharding import PartitionSpec as P

QH = 32
KVH = 4
HD = 64
G = 4
RPG = 8
P_SIZE = 2048
MOST = 1024
PREFIX_CHUNK = 512
SUFFIX_CHUNK = 256
TILE_TOKENS = 128


epsilon = 1e-05


def rotate(source, places, head_count):
    half_dim = HD // 2
    row_count = source.shape[0]
    reshaped = source.reshape(row_count, head_count, HD)
    frequency = 10000.0 ** (-(jnp.arange(half_dim, dtype=jnp.float32) * 2.0 / HD))
    angles = places.astype(jnp.float32)[:, None] * frequency[None, :]
    cos_table = jnp.cos(angles)[:, None, :]
    sine_table = jnp.sin(angles)[:, None, :]
    leading = reshaped[..., :half_dim]
    second = reshaped[..., half_dim:]
    joined = jnp.concatenate(
        [leading * cos_table - second * sine_table, second * cos_table + leading * sine_table], -1
    )
    return joined.reshape(row_count, head_count * HD)


def attend(running, queries, kv_block, allowed):
    old_max, old_sum, numerator = running
    half_width = kv_block.shape[1] // 2
    kv_heads = queries.shape[1]
    key_rows = kv_block[:, :half_width].reshape(kv_block.shape[0], kv_heads, HD)
    val_rows = kv_block[:, half_width:].reshape(kv_block.shape[0], kv_heads, HD)
    scores = jnp.einsum("qgrd,ngd->grqn", queries, key_rows, preferred_element_type=jnp.float32) * (
        1.0 / math.sqrt(HD)
    )
    scores = jnp.where(allowed[None, None], scores, -jnp.inf)
    new_max = jnp.maximum(old_max, jnp.max(scores, -1))
    factor = jnp.exp(old_max - new_max)
    weights = jnp.exp(scores - new_max[..., None])
    new_sum = old_sum * factor + jnp.sum(weights, -1)
    numerator = numerator * factor[..., None] + jnp.einsum(
        "grqn,ngd->grqd", weights.astype(jnp.bfloat16), val_rows, preferred_element_type=jnp.float32
    )
    return (new_max, new_sum, numerator)


def attention_kernel(
    table, q_ref, rg_ref, rr_ref, rp_ref, pk_ref, pv_ref, sk_ref, sv_ref, kr_ref, kp_ref,
    o_ref, m_ref, l_ref, acc_ref, *, kv_heads, prefix_chunk, suffix_chunk, chunks_per_group
):
    tile = pl.program_id(0)
    p_lo = table[4 * tile]
    p_hi = table[4 * tile + 1]
    s_lo = table[4 * tile + 2]
    s_hi = table[4 * tile + 3]
    row_group = rg_ref[...]
    row_request = rr_ref[...]
    row_place = rp_ref[...]
    for head in range(kv_heads):
        query = q_ref[head]
        m_ref[...] = jnp.full(m_ref.shape, -1e30, jnp.float32)
        l_ref[...] = jnp.zeros(l_ref.shape, jnp.float32)
        acc_ref[...] = jnp.zeros(acc_ref.shape, jnp.float32)

        def update(key, value, allowed):
            scores = lax.dot_general(
                query, key, (((1,), (1,)), ((), ())), preferred_element_type=jnp.float32
            ) * (1.0 / math.sqrt(HD))
            scores = jnp.where(allowed, scores, -jnp.inf)
            old_max = m_ref[...]
            new_max = jnp.maximum(old_max, jnp.max(scores, axis=1, keepdims=True))
            factor = jnp.exp(old_max - new_max)
            weights = jnp.exp(scores - new_max)
            l_ref[...] = l_ref[...] * factor + jnp.sum(weights, axis=1, keepdims=True)
            acc_ref[...] = acc_ref[...] * factor + jnp.dot(
                weights.astype(jnp.bfloat16), value, preferred_element_type=jnp.float32
            )
            m_ref[...] = new_max

        def prefix_step(chunk, carry):
            start = pl.multiple_of(chunk * prefix_chunk, prefix_chunk)
            key = pk_ref[head, pl.ds(start, prefix_chunk), :]
            value = pv_ref[head, pl.ds(start, prefix_chunk), :]
            update(key, value, row_group == chunk // chunks_per_group)
            return carry

        lax.fori_loop(p_lo, p_hi, prefix_step, 0)

        def suffix_step(chunk, carry):
            start = pl.multiple_of(chunk * suffix_chunk, suffix_chunk)
            key = sk_ref[head, pl.ds(start, suffix_chunk), :]
            value = sv_ref[head, pl.ds(start, suffix_chunk), :]
            key_request = kr_ref[pl.ds(chunk, 1), :]
            key_place = kp_ref[pl.ds(chunk, 1), :]
            update(key, value, (row_request == key_request) & (key_place <= row_place))
            return carry

        lax.fori_loop(s_lo, s_hi, suffix_step, 0)
        o_ref[head] = (acc_ref[...] / l_ref[...]).astype(o_ref.dtype)


def butterfly(block, axis, combine):
    count = lax.axis_size(axis)
    if count & (count - 1):
        return None
    step = 1
    while step < count:
        partner = lax.ppermute(block, axis, [(i, i ^ step) for i in range(count)])
        block = combine(block, partner)
        step *= 2
    return block


def shifted_back(block, axis, distance):
    count = lax.axis_size(axis)
    route = [(i, i + distance) for i in range(count - distance)]
    return lax.ppermute(block, axis, route)


def per_device(
    tokens, lengths, prefix_cache, attn_gain, w_query, w_keyval, w_out, final_gain, w_head
):
    token_rows = tokens.shape[0]
    model_width = tokens.shape[1]
    seq_devices = lax.axis_size("seq")
    seq_index = lax.axis_index("seq")
    mp_index = lax.axis_index("mp")
    part_width = model_width // lax.axis_size("mp")
    query_heads = w_query.shape[1] // HD
    group_size = QH // KVH
    kv_heads = max(1, query_heads // group_size)
    repeat_count = query_heads // kv_heads
    kv_first = mp_index * query_heads // group_size
    kv_width = KVH * HD
    request_count = lengths.shape[0]
    back_blocks = min(seq_devices - 1, -(-(MOST - 1) // token_rows))

    prefix_rows = prefix_cache.shape[1]
    own_prefix = jnp.concatenate(
        [
            lax.dynamic_slice_in_dim(prefix_cache, kv_first * HD, kv_heads * HD, 2),
            lax.dynamic_slice_in_dim(prefix_cache, kv_width + kv_first * HD, kv_heads * HD, 2),
        ],
        2,
    )
    own_prefix = jnp.transpose(own_prefix.reshape(G, prefix_rows, 2 * kv_heads, HD), (2, 0, 1, 3))
    all_prefix = lax.all_gather(own_prefix, "seq", axis=2, tiled=True)
    prefix_total = seq_devices * prefix_rows
    all_prefix = all_prefix.reshape(2 * kv_heads, G * prefix_total, HD)

    activations = tokens.astype(jnp.float32)
    normed = (
        activations
        * lax.rsqrt(jnp.mean(activations * activations, -1, keepdims=True) + epsilon)
        * attn_gain.astype(jnp.float32)
    ).astype(jnp.bfloat16)
    request_end = jnp.cumsum(lengths)
    starts = request_end - lengths
    position = seq_index * token_rows + jnp.arange(token_rows, dtype=jnp.int32)
    request = jnp.sum((position[:, None] >= request_end[None, :]).astype(jnp.int32), 1)
    request_table = request[:, None] == jnp.arange(request_count, dtype=jnp.int32)[None, :]
    offset = position - jnp.sum(jnp.where(request_table, starts[None, :], 0), 1)
    group_of = request // RPG
    keyval = jnp.dot(normed, w_keyval, preferred_element_type=jnp.float32)
    key_rows = rotate(keyval[:, :kv_width], P_SIZE + offset, KVH).astype(jnp.bfloat16)
    val_rows = keyval[:, kv_width:].astype(jnp.bfloat16)
    suffix_cache = jnp.concatenate([key_rows, val_rows], 1)
    own_suffix = jnp.concatenate(
        [
            lax.dynamic_slice_in_dim(key_rows, kv_first * HD, kv_heads * HD, 1),
            lax.dynamic_slice_in_dim(val_rows, kv_first * HD, kv_heads * HD, 1),
        ],
        1,
    )
    own_suffix = jnp.transpose(own_suffix.reshape(token_rows, 2 * kv_heads, HD), (1, 0, 2))
    earlier = [own_suffix] + [
        shifted_back(own_suffix, "seq", distance) for distance in range(1, back_blocks + 1)
    ]

    query_full = jnp.dot(normed, w_query, preferred_element_type=jnp.float32)
    queries = (
        rotate(query_full, P_SIZE + offset, query_heads)
        .astype(jnp.bfloat16)
        .reshape(token_rows, kv_heads, repeat_count, HD)
    )

    window_blocks = back_blocks + 1
    window_rows = window_blocks * token_rows
    window_start = (seq_index - back_blocks) * token_rows
    suffix_window = jnp.concatenate(earlier[::-1], 1)
    suffix_chunk = min(SUFFIX_CHUNK, token_rows)
    prefix_chunk = min(PREFIX_CHUNK, prefix_total)
    chunks_per_group = prefix_total // prefix_chunk
    suffix_chunks = window_rows // suffix_chunk
    key_place = window_start + jnp.arange(window_rows, dtype=jnp.int32)
    key_request = jnp.sum((key_place[:, None] >= request_end[None, :]).astype(jnp.int32), 1)
    key_request = jnp.where(key_place >= 0, key_request, -1)
    key_request = key_request.reshape(suffix_chunks, suffix_chunk)
    key_place = key_place.reshape(suffix_chunks, suffix_chunk)

    tile_tokens = min(TILE_TOKENS, token_rows)
    tile_count = token_rows // tile_tokens
    tile_rows = tile_tokens * repeat_count
    first_token = jnp.arange(tile_count, dtype=jnp.int32) * tile_tokens
    last_token = first_token + tile_tokens - 1
    p_lo = group_of[first_token] * chunks_per_group
    p_hi = (group_of[last_token] + 1) * chunks_per_group
    s_lo = jnp.maximum((starts[request[first_token]] - window_start) // suffix_chunk, 0)
    s_hi = jnp.minimum((position[last_token] - window_start) // suffix_chunk + 1, suffix_chunks)
    table = jnp.stack([p_lo, p_hi, s_lo, s_hi], 1).reshape(-1).astype(jnp.int32)

    query_rows = jnp.transpose(queries, (1, 0, 2, 3)).reshape(
        kv_heads, token_rows * repeat_count, HD
    )
    row_group = jnp.repeat(group_of, repeat_count)[:, None]
    row_request = jnp.repeat(request, repeat_count)[:, None]
    row_place = jnp.repeat(position, repeat_count)[:, None]

    def whole(shape):
        return pl.BlockSpec(shape, lambda tile, table: (0,) * len(shape))

    def half(shape, index):
        return pl.BlockSpec((kv_heads,) + shape[1:], lambda tile, table: (index, 0, 0))

    row_spec = pl.BlockSpec((tile_rows, 1), lambda tile, table: (tile, 0))
    context = pl.pallas_call(
        functools.partial(
            attention_kernel,
            kv_heads=kv_heads,
            prefix_chunk=prefix_chunk,
            suffix_chunk=suffix_chunk,
            chunks_per_group=chunks_per_group,
        ),
        grid_spec=pltpu.PrefetchScalarGridSpec(
            num_scalar_prefetch=1,
            grid=(tile_count,),
            in_specs=[
                pl.BlockSpec((kv_heads, tile_rows, HD), lambda tile, table: (0, tile, 0)),
                row_spec,
                row_spec,
                row_spec,
                half(all_prefix.shape, 0),
                half(all_prefix.shape, 1),
                half(suffix_window.shape, 0),
                half(suffix_window.shape, 1),
                whole(key_request.shape),
                whole(key_place.shape),
            ],
            out_specs=pl.BlockSpec((kv_heads, tile_rows, HD), lambda tile, table: (0, tile, 0)),
            scratch_shapes=[
                pltpu.VMEM((tile_rows, 1), jnp.float32),
                pltpu.VMEM((tile_rows, 1), jnp.float32),
                pltpu.VMEM((tile_rows, HD), jnp.float32),
            ],
        ),
        out_shape=jax.ShapeDtypeStruct((kv_heads, token_rows * repeat_count, HD), jnp.bfloat16),
    )(
        table, query_rows, row_group, row_request, row_place, all_prefix, all_prefix,
        suffix_window, suffix_window, key_request, key_place,
    )
    context = jnp.transpose(
        context.reshape(kv_heads, token_rows, repeat_count, HD), (1, 0, 2, 3)
    ).reshape(token_rows, query_heads * HD)
    mixture = jnp.dot(context, w_out, preferred_element_type=jnp.float32)
    mp_devices = lax.axis_size("mp")
    own_columns = lax.dynamic_slice_in_dim(activations, mp_index * part_width, part_width, 1)
    if mp_devices == 2:
        kept = lax.dynamic_slice_in_dim(mixture, mp_index * part_width, part_width, 1)
        sent = lax.dynamic_slice_in_dim(mixture, (1 - mp_index) * part_width, part_width, 1)
        received = lax.ppermute(sent.astype(jnp.bfloat16), "mp", [(0, 1), (1, 0)])
        hidden = (own_columns + (kept + received.astype(jnp.float32))).astype(jnp.bfloat16)
    else:
        mixture = lax.psum_scatter(
            mixture.astype(jnp.bfloat16), "mp", scatter_dimension=1, tiled=True
        ).astype(jnp.float32)
        hidden = (own_columns + mixture).astype(jnp.bfloat16)
    local_last = request_end - 1 - seq_index * token_rows
    onehot = (local_last[:, None] == jnp.arange(token_rows, dtype=jnp.int32)[None, :]).astype(
        jnp.bfloat16
    )
    last_part = jnp.dot(onehot, hidden, preferred_element_type=jnp.float32).astype(jnp.bfloat16)
    summed = butterfly(last_part, "seq", jnp.add)
    if summed is None:
        summed = lax.psum(last_part, "seq")
    last_rows = lax.all_gather(summed, "mp", axis=1, tiled=True).astype(jnp.float32)
    inv_rms = lax.rsqrt(jnp.mean(last_rows * last_rows, -1, keepdims=True) + epsilon)
    last_normed = (last_rows * final_gain.astype(jnp.float32) * inv_rms).astype(jnp.bfloat16)
    logits = jnp.dot(last_normed, w_head, preferred_element_type=jnp.float32)
    local_best = jnp.max(logits, -1)
    best_seq = butterfly(local_best, "seq", jnp.maximum)
    best_all = None if best_seq is None else butterfly(best_seq, "mp", jnp.maximum)
    greatest = lax.pmax(local_best, ("seq", "mp")) if best_all is None else best_all
    return (hidden, suffix_cache, last_normed, greatest)


def solution(mesh):
    return jax.shard_map(
        per_device,
        mesh=mesh,
        in_specs=(
            P("seq", None),
            P(),
            P(None, "seq", None),
            P(),
            P(None, "mp"),
            P(),
            P("mp", None),
            P(),
            P(None, ("seq", "mp")),
        ),
        out_specs=(P("seq", "mp"), P("seq", None), P(), P()),
        check_vma=False,
    )
```

```python
import functools
import math

import jax
import jax.numpy as jnp
from jax import lax
from jax.experimental import pallas as pl
from jax.experimental.pallas import tpu as pltpu
from jax.sharding import PartitionSpec as P

QH = 32
KVH = 4
HD = 64
G = 4
RPG = 8
P_SIZE = 2048
MOST = 1024
PREFIX_CHUNK = 512
SUFFIX_CHUNK = 256
TILE_TOKENS = 128


epsilon = 1e-05


def rotate(source, places, head_count):
    half_dim = HD // 2
    row_count = source.shape[0]
    reshaped = source.reshape(row_count, head_count, HD)
    frequency = 10000.0 ** (-(jnp.arange(half_dim, dtype=jnp.float32) * 2.0 / HD))
    angles = places.astype(jnp.float32)[:, None] * frequency[None, :]
    cos_table = jnp.cos(angles)[:, None, :]
    sine_table = jnp.sin(angles)[:, None, :]
    leading = reshaped[..., :half_dim]
    second = reshaped[..., half_dim:]
    joined = jnp.concatenate(
        [leading * cos_table - second * sine_table, second * cos_table + leading * sine_table], -1
    )
    return joined.reshape(row_count, head_count * HD)


def attend(running, queries, kv_block, allowed):
    old_max, old_sum, numerator = running
    half_width = kv_block.shape[1] // 2
    kv_heads = queries.shape[1]
    key_rows = kv_block[:, :half_width].reshape(kv_block.shape[0], kv_heads, HD)
    val_rows = kv_block[:, half_width:].reshape(kv_block.shape[0], kv_heads, HD)
    scores = jnp.einsum("qgrd,ngd->grqn", queries, key_rows, preferred_element_type=jnp.float32) * (
        1.0 / math.sqrt(HD)
    )
    scores = jnp.where(allowed[None, None], scores, -jnp.inf)
    new_max = jnp.maximum(old_max, jnp.max(scores, -1))
    factor = jnp.exp(old_max - new_max)
    weights = jnp.exp(scores - new_max[..., None])
    new_sum = old_sum * factor + jnp.sum(weights, -1)
    numerator = numerator * factor[..., None] + jnp.einsum(
        "grqn,ngd->grqd", weights.astype(jnp.bfloat16), val_rows, preferred_element_type=jnp.float32
    )
    return (new_max, new_sum, numerator)


def attention_kernel(
    table, q_ref, rg_ref, rr_ref, rp_ref, pk_ref, pv_ref, sk_ref, sv_ref, kr_ref, kp_ref,
    o_ref, m_ref, l_ref, acc_ref, *, kv_heads, prefix_chunk, suffix_chunk, chunks_per_group
):
    tile = pl.program_id(0)
    p_lo = table[4 * tile]
    p_hi = table[4 * tile + 1]
    s_lo = table[4 * tile + 2]
    s_hi = table[4 * tile + 3]
    row_group = rg_ref[...]
    row_request = rr_ref[...]
    row_place = rp_ref[...]
    for head in range(kv_heads):
        query = q_ref[head]
        m_ref[...] = jnp.full(m_ref.shape, -1e30, jnp.float32)
        l_ref[...] = jnp.zeros(l_ref.shape, jnp.float32)
        acc_ref[...] = jnp.zeros(acc_ref.shape, jnp.float32)

        def update(key, value, allowed):
            scores = lax.dot_general(
                query, key, (((1,), (1,)), ((), ())), preferred_element_type=jnp.float32
            ) * (1.0 / math.sqrt(HD))
            scores = jnp.where(allowed, scores, -jnp.inf)
            old_max = m_ref[...]
            new_max = jnp.maximum(old_max, jnp.max(scores, axis=1, keepdims=True))
            factor = jnp.exp(old_max - new_max)
            weights = jnp.exp(scores - new_max)
            l_ref[...] = l_ref[...] * factor + jnp.sum(weights, axis=1, keepdims=True)
            acc_ref[...] = acc_ref[...] * factor + jnp.dot(
                weights.astype(jnp.bfloat16), value, preferred_element_type=jnp.float32
            )
            m_ref[...] = new_max

        def prefix_step(chunk, carry):
            start = pl.multiple_of(chunk * prefix_chunk, prefix_chunk)
            key = pk_ref[head, pl.ds(start, prefix_chunk), :]
            value = pv_ref[head, pl.ds(start, prefix_chunk), :]
            update(key, value, row_group == chunk // chunks_per_group)
            return carry

        lax.fori_loop(p_lo, p_hi, prefix_step, 0)

        def suffix_step(chunk, carry):
            start = pl.multiple_of(chunk * suffix_chunk, suffix_chunk)
            key = sk_ref[head, pl.ds(start, suffix_chunk), :]
            value = sv_ref[head, pl.ds(start, suffix_chunk), :]
            key_request = kr_ref[pl.ds(chunk, 1), :]
            key_place = kp_ref[pl.ds(chunk, 1), :]
            update(key, value, (row_request == key_request) & (key_place <= row_place))
            return carry

        lax.fori_loop(s_lo, s_hi, suffix_step, 0)
        o_ref[head] = (acc_ref[...] / l_ref[...]).astype(o_ref.dtype)


def butterfly(block, axis, combine):
    count = lax.axis_size(axis)
    if count & (count - 1):
        return None
    step = 1
    while step < count:
        partner = lax.ppermute(block, axis, [(i, i ^ step) for i in range(count)])
        block = combine(block, partner)
        step *= 2
    return block


def shifted_back(block, axis, distance):
    count = lax.axis_size(axis)
    route = [(i, i + distance) for i in range(count - distance)]
    return lax.ppermute(block, axis, route)


def per_device(
    tokens, lengths, prefix_cache, attn_gain, w_query, w_keyval, w_out, final_gain, w_head
):
    token_rows = tokens.shape[0]
    model_width = tokens.shape[1]
    seq_devices = lax.axis_size("seq")
    seq_index = lax.axis_index("seq")
    mp_index = lax.axis_index("mp")
    part_width = model_width // lax.axis_size("mp")
    query_heads = w_query.shape[1] // HD
    group_size = QH // KVH
    kv_heads = max(1, query_heads // group_size)
    repeat_count = query_heads // kv_heads
    kv_first = mp_index * query_heads // group_size
    kv_width = KVH * HD
    request_count = lengths.shape[0]
    back_blocks = min(seq_devices - 1, -(-(MOST - 1) // token_rows))

    prefix_rows = prefix_cache.shape[1]
    own_prefix = jnp.concatenate(
        [
            lax.dynamic_slice_in_dim(prefix_cache, kv_first * HD, kv_heads * HD, 2),
            lax.dynamic_slice_in_dim(prefix_cache, kv_width + kv_first * HD, kv_heads * HD, 2),
        ],
        2,
    )
    own_prefix = jnp.transpose(own_prefix.reshape(G, prefix_rows, 2 * kv_heads, HD), (2, 0, 1, 3))
    all_prefix = lax.all_gather(own_prefix, "seq", axis=2, tiled=True)
    prefix_total = seq_devices * prefix_rows
    all_prefix = all_prefix.reshape(2 * kv_heads, G * prefix_total, HD)

    activations = tokens.astype(jnp.float32)
    normed = (
        activations
        * lax.rsqrt(jnp.mean(activations * activations, -1, keepdims=True) + epsilon)
        * attn_gain.astype(jnp.float32)
    ).astype(jnp.bfloat16)
    request_end = jnp.cumsum(lengths)
    starts = request_end - lengths
    position = seq_index * token_rows + jnp.arange(token_rows, dtype=jnp.int32)
    request = jnp.sum((position[:, None] >= request_end[None, :]).astype(jnp.int32), 1)
    request_table = request[:, None] == jnp.arange(request_count, dtype=jnp.int32)[None, :]
    offset = position - jnp.sum(jnp.where(request_table, starts[None, :], 0), 1)
    group_of = request // RPG
    keyval = jnp.dot(normed, w_keyval, preferred_element_type=jnp.float32)
    key_rows = rotate(keyval[:, :kv_width], P_SIZE + offset, KVH).astype(jnp.bfloat16)
    val_rows = keyval[:, kv_width:].astype(jnp.bfloat16)
    suffix_cache = jnp.concatenate([key_rows, val_rows], 1)
    own_suffix = jnp.concatenate(
        [
            lax.dynamic_slice_in_dim(key_rows, kv_first * HD, kv_heads * HD, 1),
            lax.dynamic_slice_in_dim(val_rows, kv_first * HD, kv_heads * HD, 1),
        ],
        1,
    )
    own_suffix = jnp.transpose(own_suffix.reshape(token_rows, 2 * kv_heads, HD), (1, 0, 2))
    earlier = [own_suffix] + [
        shifted_back(own_suffix, "seq", distance) for distance in range(1, back_blocks + 1)
    ]

    query_full = jnp.dot(normed, w_query, preferred_element_type=jnp.float32)
    queries = (
        rotate(query_full, P_SIZE + offset, query_heads)
        .astype(jnp.bfloat16)
        .reshape(token_rows, kv_heads, repeat_count, HD)
    )

    window_blocks = back_blocks + 1
    window_rows = window_blocks * token_rows
    window_start = (seq_index - back_blocks) * token_rows
    suffix_window = jnp.concatenate(earlier[::-1], 1)
    suffix_chunk = min(SUFFIX_CHUNK, token_rows)
    prefix_chunk = min(PREFIX_CHUNK, prefix_total)
    chunks_per_group = prefix_total // prefix_chunk
    suffix_chunks = window_rows // suffix_chunk
    key_place = window_start + jnp.arange(window_rows, dtype=jnp.int32)
    key_request = jnp.sum((key_place[:, None] >= request_end[None, :]).astype(jnp.int32), 1)
    key_request = jnp.where(key_place >= 0, key_request, -1)
    key_request = key_request.reshape(suffix_chunks, suffix_chunk)
    key_place = key_place.reshape(suffix_chunks, suffix_chunk)

    tile_tokens = min(TILE_TOKENS, token_rows)
    tile_count = token_rows // tile_tokens
    tile_rows = tile_tokens * repeat_count
    first_token = jnp.arange(tile_count, dtype=jnp.int32) * tile_tokens
    last_token = first_token + tile_tokens - 1
    p_lo = group_of[first_token] * chunks_per_group
    p_hi = (group_of[last_token] + 1) * chunks_per_group
    s_lo = jnp.maximum((starts[request[first_token]] - window_start) // suffix_chunk, 0)
    s_hi = jnp.minimum((position[last_token] - window_start) // suffix_chunk + 1, suffix_chunks)
    table = jnp.stack([p_lo, p_hi, s_lo, s_hi], 1).reshape(-1).astype(jnp.int32)

    query_rows = jnp.transpose(queries, (1, 0, 2, 3)).reshape(
        kv_heads, token_rows * repeat_count, HD
    )
    row_group = jnp.repeat(group_of, repeat_count)[:, None]
    row_request = jnp.repeat(request, repeat_count)[:, None]
    row_place = jnp.repeat(position, repeat_count)[:, None]

    def whole(shape):
        return pl.BlockSpec(shape, lambda tile, table: (0,) * len(shape))

    def half(shape, index):
        return pl.BlockSpec((kv_heads,) + shape[1:], lambda tile, table: (index, 0, 0))

    row_spec = pl.BlockSpec((tile_rows, 1), lambda tile, table: (tile, 0))
    context = pl.pallas_call(
        functools.partial(
            attention_kernel,
            kv_heads=kv_heads,
            prefix_chunk=prefix_chunk,
            suffix_chunk=suffix_chunk,
            chunks_per_group=chunks_per_group,
        ),
        grid_spec=pltpu.PrefetchScalarGridSpec(
            num_scalar_prefetch=1,
            grid=(tile_count,),
            in_specs=[
                pl.BlockSpec((kv_heads, tile_rows, HD), lambda tile, table: (0, tile, 0)),
                row_spec,
                row_spec,
                row_spec,
                half(all_prefix.shape, 0),
                half(all_prefix.shape, 1),
                half(suffix_window.shape, 0),
                half(suffix_window.shape, 1),
                whole(key_request.shape),
                whole(key_place.shape),
            ],
            out_specs=pl.BlockSpec((kv_heads, tile_rows, HD), lambda tile, table: (0, tile, 0)),
            scratch_shapes=[
                pltpu.VMEM((tile_rows, 1), jnp.float32),
                pltpu.VMEM((tile_rows, 1), jnp.float32),
                pltpu.VMEM((tile_rows, HD), jnp.float32),
            ],
        ),
        out_shape=jax.ShapeDtypeStruct((kv_heads, token_rows * repeat_count, HD), jnp.bfloat16),
    )(
        table, query_rows, row_group, row_request, row_place, all_prefix, all_prefix,
        suffix_window, suffix_window, key_request, key_place,
    )
    context = jnp.transpose(
        context.reshape(kv_heads, token_rows, repeat_count, HD), (1, 0, 2, 3)
    ).reshape(token_rows, query_heads * HD)
    local_last = request_end - 1 - seq_index * token_rows
    onehot = (local_last[:, None] == jnp.arange(token_rows, dtype=jnp.int32)[None, :]).astype(
        jnp.bfloat16
    )
    context_last = jnp.dot(onehot, context, preferred_element_type=jnp.float32)
    tokens_last = jnp.dot(onehot, tokens, preferred_element_type=jnp.float32)
    last_part = jnp.dot(
        context_last.astype(jnp.bfloat16), w_out, preferred_element_type=jnp.float32
    ) + jnp.where(mp_index == 0, tokens_last, 0.0)
    mixture = jnp.dot(context, w_out, preferred_element_type=jnp.float32)
    mp_devices = lax.axis_size("mp")
    own_columns = lax.dynamic_slice_in_dim(activations, mp_index * part_width, part_width, 1)
    if mp_devices == 2:
        kept = lax.dynamic_slice_in_dim(mixture, mp_index * part_width, part_width, 1)
        sent = lax.dynamic_slice_in_dim(mixture, (1 - mp_index) * part_width, part_width, 1)
        received = lax.ppermute(sent.astype(jnp.bfloat16), "mp", [(0, 1), (1, 0)])
        hidden = (own_columns + (kept + received.astype(jnp.float32))).astype(jnp.bfloat16)
    else:
        mixture = lax.psum_scatter(
            mixture.astype(jnp.bfloat16), "mp", scatter_dimension=1, tiled=True
        ).astype(jnp.float32)
        hidden = (own_columns + mixture).astype(jnp.bfloat16)
    last_rows = butterfly(last_part, "seq", jnp.add)
    last_rows = lax.psum(last_part, "seq") if last_rows is None else last_rows
    summed = butterfly(last_rows, "mp", jnp.add)
    last_rows = lax.psum(last_rows, "mp") if summed is None else summed
    last_rows = last_rows.astype(jnp.bfloat16).astype(jnp.float32)
    inv_rms = lax.rsqrt(jnp.mean(last_rows * last_rows, -1, keepdims=True) + epsilon)
    last_normed = (last_rows * final_gain.astype(jnp.float32) * inv_rms).astype(jnp.bfloat16)
    logits = jnp.dot(last_normed, w_head, preferred_element_type=jnp.float32)
    local_best = jnp.max(logits, -1)
    best_seq = butterfly(local_best, "seq", jnp.maximum)
    best_all = None if best_seq is None else butterfly(best_seq, "mp", jnp.maximum)
    greatest = lax.pmax(local_best, ("seq", "mp")) if best_all is None else best_all
    return (hidden, suffix_cache, last_normed, greatest)


def solution(mesh):
    return jax.shard_map(
        per_device,
        mesh=mesh,
        in_specs=(
            P("seq", None),
            P(),
            P(None, "seq", None),
            P(),
            P(None, "mp"),
            P(),
            P("mp", None),
            P(),
            P(None, ("seq", "mp")),
        ),
        out_specs=(P("seq", "mp"), P("seq", None), P(), P()),
        check_vma=False,
    )
```

```python
import functools
import math

import jax
import jax.numpy as jnp
from jax import lax
from jax.experimental import pallas as pl
from jax.experimental.pallas import tpu as pltpu
from jax.sharding import PartitionSpec as P

QH = 32
KVH = 4
HD = 64
G = 4
RPG = 8
P_SIZE = 2048
MOST = 1024
PREFIX_CHUNK = 512
SUFFIX_CHUNK = 256
TILE_TOKENS = 128


epsilon = 1e-05


def rotate(source, places, head_count):
    half_dim = HD // 2
    row_count = source.shape[0]
    reshaped = source.reshape(row_count, head_count, HD)
    frequency = 10000.0 ** (-(jnp.arange(half_dim, dtype=jnp.float32) * 2.0 / HD))
    angles = places.astype(jnp.float32)[:, None] * frequency[None, :]
    cos_table = jnp.cos(angles)[:, None, :]
    sine_table = jnp.sin(angles)[:, None, :]
    leading = reshaped[..., :half_dim]
    second = reshaped[..., half_dim:]
    joined = jnp.concatenate(
        [leading * cos_table - second * sine_table, second * cos_table + leading * sine_table], -1
    )
    return joined.reshape(row_count, head_count * HD)


def attend(running, queries, kv_block, allowed):
    old_max, old_sum, numerator = running
    half_width = kv_block.shape[1] // 2
    kv_heads = queries.shape[1]
    key_rows = kv_block[:, :half_width].reshape(kv_block.shape[0], kv_heads, HD)
    val_rows = kv_block[:, half_width:].reshape(kv_block.shape[0], kv_heads, HD)
    scores = jnp.einsum("qgrd,ngd->grqn", queries, key_rows, preferred_element_type=jnp.float32) * (
        1.0 / math.sqrt(HD)
    )
    scores = jnp.where(allowed[None, None], scores, -jnp.inf)
    new_max = jnp.maximum(old_max, jnp.max(scores, -1))
    factor = jnp.exp(old_max - new_max)
    weights = jnp.exp(scores - new_max[..., None])
    new_sum = old_sum * factor + jnp.sum(weights, -1)
    numerator = numerator * factor[..., None] + jnp.einsum(
        "grqn,ngd->grqd", weights.astype(jnp.bfloat16), val_rows, preferred_element_type=jnp.float32
    )
    return (new_max, new_sum, numerator)


def attention_kernel(
    table, q_ref, rg_ref, rr_ref, rp_ref, pk_ref, pv_ref, sk_ref, sv_ref, kr_ref, kp_ref,
    o_ref, m_ref, l_ref, acc_ref, *, kv_heads, prefix_chunk, suffix_chunk, parts_per_group
):
    tile = pl.program_id(0)
    p_lo = table[4 * tile]
    p_hi = table[4 * tile + 1]
    s_lo = table[4 * tile + 2]
    s_hi = table[4 * tile + 3]
    row_group = rg_ref[...]
    row_request = rr_ref[...]
    row_place = rp_ref[...]
    for head in range(kv_heads):
        query = q_ref[head]
        m_ref[...] = jnp.full(m_ref.shape, -1e30, jnp.float32)
        l_ref[...] = jnp.zeros(l_ref.shape, jnp.float32)
        acc_ref[...] = jnp.zeros(acc_ref.shape, jnp.float32)

        def update(key, value, allowed):
            scores = lax.dot_general(
                query, key, (((1,), (1,)), ((), ())), preferred_element_type=jnp.float32
            ) * (1.0 / math.sqrt(HD))
            scores = jnp.where(allowed, scores, -jnp.inf)
            old_max = m_ref[...]
            new_max = jnp.maximum(old_max, jnp.max(scores, axis=1, keepdims=True))
            factor = jnp.exp(old_max - new_max)
            weights = jnp.exp(scores - new_max)
            l_ref[...] = l_ref[...] * factor + jnp.sum(weights, axis=1, keepdims=True)
            acc_ref[...] = acc_ref[...] * factor + jnp.dot(
                weights.astype(jnp.bfloat16), value, preferred_element_type=jnp.float32
            )
            m_ref[...] = new_max

        def prefix_step(group, carry):
            allowed = row_group == group
            for part in range(parts_per_group):
                lanes = slice(part * prefix_chunk, (part + 1) * prefix_chunk)
                key_t = pk_ref[group, head, :, lanes]
                value_t = pv_ref[group, head, :, lanes]
                scores = jnp.dot(query, key_t, preferred_element_type=jnp.float32) * (
                    1.0 / math.sqrt(HD)
                )
                scores = jnp.where(allowed, scores, -jnp.inf)
                old_max = m_ref[...]
                new_max = jnp.maximum(old_max, jnp.max(scores, axis=1, keepdims=True))
                factor = jnp.exp(old_max - new_max)
                weights = jnp.exp(scores - new_max)
                l_ref[...] = l_ref[...] * factor + jnp.sum(weights, axis=1, keepdims=True)
                acc_ref[...] = acc_ref[...] * factor + lax.dot_general(
                    weights.astype(jnp.bfloat16), value_t, (((1,), (1,)), ((), ())),
                    preferred_element_type=jnp.float32,
                )
                m_ref[...] = new_max
            return carry

        lax.fori_loop(p_lo, p_hi, prefix_step, 0)

        def suffix_step(chunk, carry):
            start = pl.multiple_of(chunk * suffix_chunk, suffix_chunk)
            key = sk_ref[head, pl.ds(start, suffix_chunk), :]
            value = sv_ref[head, pl.ds(start, suffix_chunk), :]
            key_request = kr_ref[pl.ds(chunk, 1), :]
            key_place = kp_ref[pl.ds(chunk, 1), :]
            update(key, value, (row_request == key_request) & (key_place <= row_place))
            return carry

        lax.fori_loop(s_lo, s_hi, suffix_step, 0)
        o_ref[head] = (acc_ref[...] / l_ref[...]).astype(o_ref.dtype)


def butterfly(block, axis, combine):
    count = lax.axis_size(axis)
    if count & (count - 1):
        return None
    step = 1
    while step < count:
        partner = lax.ppermute(block, axis, [(i, i ^ step) for i in range(count)])
        block = combine(block, partner)
        step *= 2
    return block


def shifted_back(block, axis, distance):
    count = lax.axis_size(axis)
    route = [(i, i + distance) for i in range(count - distance)]
    return lax.ppermute(block, axis, route)


def per_device(
    tokens, lengths, prefix_cache, attn_gain, w_query, w_keyval, w_out, final_gain, w_head
):
    token_rows = tokens.shape[0]
    model_width = tokens.shape[1]
    seq_devices = lax.axis_size("seq")
    seq_index = lax.axis_index("seq")
    mp_index = lax.axis_index("mp")
    part_width = model_width // lax.axis_size("mp")
    query_heads = w_query.shape[1] // HD
    group_size = QH // KVH
    kv_heads = max(1, query_heads // group_size)
    repeat_count = query_heads // kv_heads
    kv_first = mp_index * query_heads // group_size
    kv_width = KVH * HD
    request_count = lengths.shape[0]
    back_blocks = min(seq_devices - 1, -(-(MOST - 1) // token_rows))

    prefix_rows = prefix_cache.shape[1]
    own_prefix = jnp.concatenate(
        [
            lax.dynamic_slice_in_dim(prefix_cache, kv_first * HD, kv_heads * HD, 2),
            lax.dynamic_slice_in_dim(prefix_cache, kv_width + kv_first * HD, kv_heads * HD, 2),
        ],
        2,
    )
    own_prefix = jnp.transpose(own_prefix.reshape(G, prefix_rows, 2 * kv_heads, HD), (2, 0, 1, 3))
    all_prefix = lax.all_gather(own_prefix, "seq", axis=2, tiled=True)
    prefix_total = seq_devices * prefix_rows
    all_prefix = jnp.transpose(all_prefix, (1, 0, 3, 2))

    activations = tokens.astype(jnp.float32)
    normed = (
        activations
        * lax.rsqrt(jnp.mean(activations * activations, -1, keepdims=True) + epsilon)
        * attn_gain.astype(jnp.float32)
    ).astype(jnp.bfloat16)
    request_end = jnp.cumsum(lengths)
    starts = request_end - lengths
    position = seq_index * token_rows + jnp.arange(token_rows, dtype=jnp.int32)
    request = jnp.sum((position[:, None] >= request_end[None, :]).astype(jnp.int32), 1)
    request_table = request[:, None] == jnp.arange(request_count, dtype=jnp.int32)[None, :]
    offset = position - jnp.sum(jnp.where(request_table, starts[None, :], 0), 1)
    group_of = request // RPG
    keyval = jnp.dot(normed, w_keyval, preferred_element_type=jnp.float32)
    key_rows = rotate(keyval[:, :kv_width], P_SIZE + offset, KVH).astype(jnp.bfloat16)
    val_rows = keyval[:, kv_width:].astype(jnp.bfloat16)
    suffix_cache = jnp.concatenate([key_rows, val_rows], 1)
    own_suffix = jnp.concatenate(
        [
            lax.dynamic_slice_in_dim(key_rows, kv_first * HD, kv_heads * HD, 1),
            lax.dynamic_slice_in_dim(val_rows, kv_first * HD, kv_heads * HD, 1),
        ],
        1,
    )
    own_suffix = jnp.transpose(own_suffix.reshape(token_rows, 2 * kv_heads, HD), (1, 0, 2))
    earlier = [own_suffix] + [
        shifted_back(own_suffix, "seq", distance) for distance in range(1, back_blocks + 1)
    ]

    query_full = jnp.dot(normed, w_query, preferred_element_type=jnp.float32)
    queries = (
        rotate(query_full, P_SIZE + offset, query_heads)
        .astype(jnp.bfloat16)
        .reshape(token_rows, kv_heads, repeat_count, HD)
    )

    window_blocks = back_blocks + 1
    window_rows = window_blocks * token_rows
    window_start = (seq_index - back_blocks) * token_rows
    suffix_window = jnp.concatenate(earlier[::-1], 1)
    suffix_chunk = min(SUFFIX_CHUNK, token_rows)
    prefix_chunk = min(PREFIX_CHUNK, prefix_total)
    chunks_per_group = prefix_total // prefix_chunk
    suffix_chunks = window_rows // suffix_chunk
    key_place = window_start + jnp.arange(window_rows, dtype=jnp.int32)
    key_request = jnp.sum((key_place[:, None] >= request_end[None, :]).astype(jnp.int32), 1)
    key_request = jnp.where(key_place >= 0, key_request, -1)
    key_request = key_request.reshape(suffix_chunks, suffix_chunk)
    key_place = key_place.reshape(suffix_chunks, suffix_chunk)

    tile_tokens = min(TILE_TOKENS, token_rows)
    tile_count = token_rows // tile_tokens
    tile_rows = tile_tokens * repeat_count
    first_token = jnp.arange(tile_count, dtype=jnp.int32) * tile_tokens
    last_token = first_token + tile_tokens - 1
    p_lo = group_of[first_token]
    p_hi = group_of[last_token] + 1
    s_lo = jnp.maximum((starts[request[first_token]] - window_start) // suffix_chunk, 0)
    s_hi = jnp.minimum((position[last_token] - window_start) // suffix_chunk + 1, suffix_chunks)
    table = jnp.stack([p_lo, p_hi, s_lo, s_hi], 1).reshape(-1).astype(jnp.int32)

    query_rows = jnp.transpose(queries, (1, 0, 2, 3)).reshape(
        kv_heads, token_rows * repeat_count, HD
    )
    row_group = jnp.repeat(group_of, repeat_count)[:, None]
    row_request = jnp.repeat(request, repeat_count)[:, None]
    row_place = jnp.repeat(position, repeat_count)[:, None]

    def whole(shape):
        return pl.BlockSpec(shape, lambda tile, table: (0,) * len(shape))

    def half(shape, index):
        return pl.BlockSpec((kv_heads,) + shape[1:], lambda tile, table: (index, 0, 0))

    def prefix_half(index):
        shape = (G, kv_heads, HD, prefix_total)
        return pl.BlockSpec(shape, lambda tile, table: (0, index, 0, 0))

    row_spec = pl.BlockSpec((tile_rows, 1), lambda tile, table: (tile, 0))
    context = pl.pallas_call(
        functools.partial(
            attention_kernel,
            kv_heads=kv_heads,
            prefix_chunk=prefix_chunk,
            suffix_chunk=suffix_chunk,
            parts_per_group=chunks_per_group,
        ),
        grid_spec=pltpu.PrefetchScalarGridSpec(
            num_scalar_prefetch=1,
            grid=(tile_count,),
            in_specs=[
                pl.BlockSpec((kv_heads, tile_rows, HD), lambda tile, table: (0, tile, 0)),
                row_spec,
                row_spec,
                row_spec,
                prefix_half(0),
                prefix_half(1),
                half(suffix_window.shape, 0),
                half(suffix_window.shape, 1),
                whole(key_request.shape),
                whole(key_place.shape),
            ],
            out_specs=pl.BlockSpec((kv_heads, tile_rows, HD), lambda tile, table: (0, tile, 0)),
            scratch_shapes=[
                pltpu.VMEM((tile_rows, 1), jnp.float32),
                pltpu.VMEM((tile_rows, 1), jnp.float32),
                pltpu.VMEM((tile_rows, HD), jnp.float32),
            ],
        ),
        out_shape=jax.ShapeDtypeStruct((kv_heads, token_rows * repeat_count, HD), jnp.bfloat16),
    )(
        table, query_rows, row_group, row_request, row_place, all_prefix, all_prefix,
        suffix_window, suffix_window, key_request, key_place,
    )
    context = jnp.transpose(
        context.reshape(kv_heads, token_rows, repeat_count, HD), (1, 0, 2, 3)
    ).reshape(token_rows, query_heads * HD)
    mixture = jnp.dot(context, w_out, preferred_element_type=jnp.float32)
    mp_devices = lax.axis_size("mp")
    own_columns = lax.dynamic_slice_in_dim(activations, mp_index * part_width, part_width, 1)
    if mp_devices == 2:
        kept = lax.dynamic_slice_in_dim(mixture, mp_index * part_width, part_width, 1)
        sent = lax.dynamic_slice_in_dim(mixture, (1 - mp_index) * part_width, part_width, 1)
        received = lax.ppermute(sent.astype(jnp.bfloat16), "mp", [(0, 1), (1, 0)])
        hidden = (own_columns + (kept + received.astype(jnp.float32))).astype(jnp.bfloat16)
    else:
        mixture = lax.psum_scatter(
            mixture.astype(jnp.bfloat16), "mp", scatter_dimension=1, tiled=True
        ).astype(jnp.float32)
        hidden = (own_columns + mixture).astype(jnp.bfloat16)
    local_last = request_end - 1 - seq_index * token_rows
    onehot = (local_last[:, None] == jnp.arange(token_rows, dtype=jnp.int32)[None, :]).astype(
        jnp.bfloat16
    )
    last_part = jnp.dot(onehot, hidden, preferred_element_type=jnp.float32).astype(jnp.bfloat16)
    summed = butterfly(last_part, "seq", jnp.add)
    if summed is None:
        summed = lax.psum(last_part, "seq")
    last_rows = lax.all_gather(summed, "mp", axis=1, tiled=True).astype(jnp.float32)
    inv_rms = lax.rsqrt(jnp.mean(last_rows * last_rows, -1, keepdims=True) + epsilon)
    last_normed = (last_rows * final_gain.astype(jnp.float32) * inv_rms).astype(jnp.bfloat16)
    logits = jnp.dot(last_normed, w_head, preferred_element_type=jnp.float32)
    local_best = jnp.max(logits, -1)
    best_seq = butterfly(local_best, "seq", jnp.maximum)
    best_all = None if best_seq is None else butterfly(best_seq, "mp", jnp.maximum)
    greatest = lax.pmax(local_best, ("seq", "mp")) if best_all is None else best_all
    return (hidden, suffix_cache, last_normed, greatest)


def solution(mesh):
    return jax.shard_map(
        per_device,
        mesh=mesh,
        in_specs=(
            P("seq", None),
            P(),
            P(None, "seq", None),
            P(),
            P(None, "mp"),
            P(),
            P("mp", None),
            P(),
            P(None, ("seq", "mp")),
        ),
        out_specs=(P("seq", "mp"), P("seq", None), P(), P()),
        check_vma=False,
    )
```

```python
import functools
import math

import jax
import jax.numpy as jnp
from jax import lax
from jax.experimental import pallas as pl
from jax.experimental.pallas import tpu as pltpu
from jax.sharding import PartitionSpec as P

QH = 32
KVH = 4
HD = 64
G = 4
RPG = 8
P_SIZE = 2048
MOST = 1024
PREFIX_CHUNK = 512
SUFFIX_CHUNK = 256
TILE_TOKENS = 128


epsilon = 1e-05


def rotate(source, places, head_count):
    half_dim = HD // 2
    row_count = source.shape[0]
    reshaped = source.reshape(row_count, head_count, HD)
    frequency = 10000.0 ** (-(jnp.arange(half_dim, dtype=jnp.float32) * 2.0 / HD))
    angles = places.astype(jnp.float32)[:, None] * frequency[None, :]
    cos_table = jnp.cos(angles)[:, None, :]
    sine_table = jnp.sin(angles)[:, None, :]
    leading = reshaped[..., :half_dim]
    second = reshaped[..., half_dim:]
    joined = jnp.concatenate(
        [leading * cos_table - second * sine_table, second * cos_table + leading * sine_table], -1
    )
    return joined.reshape(row_count, head_count * HD)


def attend(running, queries, kv_block, allowed):
    old_max, old_sum, numerator = running
    half_width = kv_block.shape[1] // 2
    kv_heads = queries.shape[1]
    key_rows = kv_block[:, :half_width].reshape(kv_block.shape[0], kv_heads, HD)
    val_rows = kv_block[:, half_width:].reshape(kv_block.shape[0], kv_heads, HD)
    scores = jnp.einsum("qgrd,ngd->grqn", queries, key_rows, preferred_element_type=jnp.float32) * (
        1.0 / math.sqrt(HD)
    )
    scores = jnp.where(allowed[None, None], scores, -jnp.inf)
    new_max = jnp.maximum(old_max, jnp.max(scores, -1))
    factor = jnp.exp(old_max - new_max)
    weights = jnp.exp(scores - new_max[..., None])
    new_sum = old_sum * factor + jnp.sum(weights, -1)
    numerator = numerator * factor[..., None] + jnp.einsum(
        "grqn,ngd->grqd", weights.astype(jnp.bfloat16), val_rows, preferred_element_type=jnp.float32
    )
    return (new_max, new_sum, numerator)


def online_update(m_ref, l_ref, acc_ref, head, scores, value, value_contract):
    old_max = m_ref[head]
    new_max = jnp.maximum(old_max, jnp.max(scores, axis=1, keepdims=True))
    factor = jnp.exp(old_max - new_max)
    weights = jnp.exp(scores - new_max)
    l_ref[head] = l_ref[head] * factor + jnp.sum(weights, axis=1, keepdims=True)
    acc_ref[head] = acc_ref[head] * factor + lax.dot_general(
        weights.astype(jnp.bfloat16), value, (((1,), (value_contract,)), ((), ())),
        preferred_element_type=jnp.float32,
    )
    m_ref[head] = new_max


def suffix_kernel(
    table, q_ref, rr_ref, rp_ref, sk_ref, sv_ref, kr_ref, kp_ref, m_ref, l_ref, acc_ref,
    *, kv_heads, suffix_chunk
):
    tile = pl.program_id(0)
    s_lo = table[4 * tile + 2]
    s_hi = table[4 * tile + 3]
    row_request = rr_ref[...]
    row_place = rp_ref[...]
    for head in range(kv_heads):
        query = q_ref[head]
        m_ref[head] = jnp.full(m_ref.shape[1:], -1e30, jnp.float32)
        l_ref[head] = jnp.zeros(l_ref.shape[1:], jnp.float32)
        acc_ref[head] = jnp.zeros(acc_ref.shape[1:], jnp.float32)

        def suffix_step(chunk, carry):
            start = pl.multiple_of(chunk * suffix_chunk, suffix_chunk)
            key = sk_ref[head, pl.ds(start, suffix_chunk), :]
            value = sv_ref[head, pl.ds(start, suffix_chunk), :]
            key_request = kr_ref[pl.ds(chunk, 1), :]
            key_place = kp_ref[pl.ds(chunk, 1), :]
            scores = lax.dot_general(
                query, key, (((1,), (1,)), ((), ())), preferred_element_type=jnp.float32
            ) * (1.0 / math.sqrt(HD))
            allowed = (row_request == key_request) & (key_place <= row_place)
            scores = jnp.where(allowed, scores, -jnp.inf)
            online_update(m_ref, l_ref, acc_ref, head, scores, value, 0)
            return carry

        lax.fori_loop(s_lo, s_hi, suffix_step, 0)


def prefix_kernel(
    table, q_ref, rg_ref, pk_ref, pv_ref, mi_ref, li_ref, ai_ref, o_ref, m_ref, l_ref, acc_ref,
    *, kv_heads, prefix_chunk, parts_per_group
):
    tile = pl.program_id(0)
    p_lo = table[4 * tile]
    p_hi = table[4 * tile + 1]
    row_group = rg_ref[...]
    for head in range(kv_heads):
        query = q_ref[head]
        m_ref[0] = mi_ref[head]
        l_ref[0] = li_ref[head]
        acc_ref[0] = ai_ref[head]

        def prefix_step(group, carry):
            allowed = row_group == group
            for part in range(parts_per_group):
                lanes = slice(part * prefix_chunk, (part + 1) * prefix_chunk)
                key_t = pk_ref[group, head, :, lanes]
                value_t = pv_ref[group, head, :, lanes]
                scores = jnp.dot(query, key_t, preferred_element_type=jnp.float32) * (
                    1.0 / math.sqrt(HD)
                )
                scores = jnp.where(allowed, scores, -jnp.inf)
                online_update(m_ref, l_ref, acc_ref, 0, scores, value_t, 1)
            return carry

        lax.fori_loop(p_lo, p_hi, prefix_step, 0)
        o_ref[head] = (acc_ref[0] / l_ref[0]).astype(o_ref.dtype)


def butterfly(block, axis, combine):
    count = lax.axis_size(axis)
    if count & (count - 1):
        return None
    step = 1
    while step < count:
        partner = lax.ppermute(block, axis, [(i, i ^ step) for i in range(count)])
        block = combine(block, partner)
        step *= 2
    return block


def shifted_back(block, axis, distance):
    count = lax.axis_size(axis)
    route = [(i, i + distance) for i in range(count - distance)]
    return lax.ppermute(block, axis, route)


def per_device(
    tokens, lengths, prefix_cache, attn_gain, w_query, w_keyval, w_out, final_gain, w_head
):
    token_rows = tokens.shape[0]
    model_width = tokens.shape[1]
    seq_devices = lax.axis_size("seq")
    seq_index = lax.axis_index("seq")
    mp_index = lax.axis_index("mp")
    part_width = model_width // lax.axis_size("mp")
    query_heads = w_query.shape[1] // HD
    group_size = QH // KVH
    kv_heads = max(1, query_heads // group_size)
    repeat_count = query_heads // kv_heads
    kv_first = mp_index * query_heads // group_size
    kv_width = KVH * HD
    request_count = lengths.shape[0]
    back_blocks = min(seq_devices - 1, -(-(MOST - 1) // token_rows))

    prefix_rows = prefix_cache.shape[1]
    own_prefix = jnp.concatenate(
        [
            lax.dynamic_slice_in_dim(prefix_cache, kv_first * HD, kv_heads * HD, 2),
            lax.dynamic_slice_in_dim(prefix_cache, kv_width + kv_first * HD, kv_heads * HD, 2),
        ],
        2,
    )
    own_prefix = jnp.transpose(own_prefix.reshape(G, prefix_rows, 2 * kv_heads, HD), (2, 0, 1, 3))
    all_prefix = lax.all_gather(own_prefix, "seq", axis=2, tiled=True)
    prefix_total = seq_devices * prefix_rows
    all_prefix = jnp.transpose(all_prefix, (1, 0, 3, 2))

    activations = tokens.astype(jnp.float32)
    normed = (
        activations
        * lax.rsqrt(jnp.mean(activations * activations, -1, keepdims=True) + epsilon)
        * attn_gain.astype(jnp.float32)
    ).astype(jnp.bfloat16)
    request_end = jnp.cumsum(lengths)
    starts = request_end - lengths
    position = seq_index * token_rows + jnp.arange(token_rows, dtype=jnp.int32)
    request = jnp.sum((position[:, None] >= request_end[None, :]).astype(jnp.int32), 1)
    request_table = request[:, None] == jnp.arange(request_count, dtype=jnp.int32)[None, :]
    offset = position - jnp.sum(jnp.where(request_table, starts[None, :], 0), 1)
    group_of = request // RPG
    keyval = jnp.dot(normed, w_keyval, preferred_element_type=jnp.float32)
    key_rows = rotate(keyval[:, :kv_width], P_SIZE + offset, KVH).astype(jnp.bfloat16)
    val_rows = keyval[:, kv_width:].astype(jnp.bfloat16)
    suffix_cache = jnp.concatenate([key_rows, val_rows], 1)
    own_suffix = jnp.concatenate(
        [
            lax.dynamic_slice_in_dim(key_rows, kv_first * HD, kv_heads * HD, 1),
            lax.dynamic_slice_in_dim(val_rows, kv_first * HD, kv_heads * HD, 1),
        ],
        1,
    )
    own_suffix = jnp.transpose(own_suffix.reshape(token_rows, 2 * kv_heads, HD), (1, 0, 2))
    earlier = [own_suffix] + [
        shifted_back(own_suffix, "seq", distance) for distance in range(1, back_blocks + 1)
    ]

    query_full = jnp.dot(normed, w_query, preferred_element_type=jnp.float32)
    queries = (
        rotate(query_full, P_SIZE + offset, query_heads)
        .astype(jnp.bfloat16)
        .reshape(token_rows, kv_heads, repeat_count, HD)
    )

    window_blocks = back_blocks + 1
    window_rows = window_blocks * token_rows
    window_start = (seq_index - back_blocks) * token_rows
    suffix_window = jnp.concatenate(earlier[::-1], 1)
    suffix_chunk = min(SUFFIX_CHUNK, token_rows)
    prefix_chunk = min(PREFIX_CHUNK, prefix_total)
    chunks_per_group = prefix_total // prefix_chunk
    suffix_chunks = window_rows // suffix_chunk
    key_place = window_start + jnp.arange(window_rows, dtype=jnp.int32)
    key_request = jnp.sum((key_place[:, None] >= request_end[None, :]).astype(jnp.int32), 1)
    key_request = jnp.where(key_place >= 0, key_request, -1)
    key_request = key_request.reshape(suffix_chunks, suffix_chunk)
    key_place = key_place.reshape(suffix_chunks, suffix_chunk)

    tile_tokens = min(TILE_TOKENS, token_rows)
    tile_count = token_rows // tile_tokens
    tile_rows = tile_tokens * repeat_count
    first_token = jnp.arange(tile_count, dtype=jnp.int32) * tile_tokens
    last_token = first_token + tile_tokens - 1
    p_lo = group_of[first_token]
    p_hi = group_of[last_token] + 1
    s_lo = jnp.maximum((starts[request[first_token]] - window_start) // suffix_chunk, 0)
    s_hi = jnp.minimum((position[last_token] - window_start) // suffix_chunk + 1, suffix_chunks)
    table = jnp.stack([p_lo, p_hi, s_lo, s_hi], 1).reshape(-1).astype(jnp.int32)

    query_rows = jnp.transpose(queries, (1, 0, 2, 3)).reshape(
        kv_heads, token_rows * repeat_count, HD
    )
    row_group = jnp.repeat(group_of, repeat_count)[:, None]
    row_request = jnp.repeat(request, repeat_count)[:, None]
    row_place = jnp.repeat(position, repeat_count)[:, None]

    def whole(shape):
        return pl.BlockSpec(shape, lambda tile, table: (0,) * len(shape))

    def half(shape, index):
        return pl.BlockSpec((kv_heads,) + shape[1:], lambda tile, table: (index, 0, 0))

    def prefix_half(index):
        shape = (G, kv_heads, HD, prefix_total)
        return pl.BlockSpec(shape, lambda tile, table: (0, index, 0, 0))

    row_spec = pl.BlockSpec((tile_rows, 1), lambda tile, table: (tile, 0))
    rows_total = token_rows * repeat_count
    state_shapes = [
        jax.ShapeDtypeStruct((kv_heads, rows_total, 1), jnp.float32),
        jax.ShapeDtypeStruct((kv_heads, rows_total, 1), jnp.float32),
        jax.ShapeDtypeStruct((kv_heads, rows_total, HD), jnp.float32),
    ]
    state_specs = [
        pl.BlockSpec((kv_heads, tile_rows, 1), lambda tile, table: (0, tile, 0)),
        pl.BlockSpec((kv_heads, tile_rows, 1), lambda tile, table: (0, tile, 0)),
        pl.BlockSpec((kv_heads, tile_rows, HD), lambda tile, table: (0, tile, 0)),
    ]
    query_spec = pl.BlockSpec((kv_heads, tile_rows, HD), lambda tile, table: (0, tile, 0))
    state = pl.pallas_call(
        functools.partial(suffix_kernel, kv_heads=kv_heads, suffix_chunk=suffix_chunk),
        grid_spec=pltpu.PrefetchScalarGridSpec(
            num_scalar_prefetch=1,
            grid=(tile_count,),
            in_specs=[
                query_spec,
                row_spec,
                row_spec,
                half(suffix_window.shape, 0),
                half(suffix_window.shape, 1),
                whole(key_request.shape),
                whole(key_place.shape),
            ],
            out_specs=state_specs,
        ),
        out_shape=state_shapes,
    )(table, query_rows, row_request, row_place, suffix_window, suffix_window, key_request, key_place)
    context = pl.pallas_call(
        functools.partial(
            prefix_kernel,
            kv_heads=kv_heads,
            prefix_chunk=prefix_chunk,
            parts_per_group=chunks_per_group,
        ),
        grid_spec=pltpu.PrefetchScalarGridSpec(
            num_scalar_prefetch=1,
            grid=(tile_count,),
            in_specs=[query_spec, row_spec, prefix_half(0), prefix_half(1)] + state_specs,
            out_specs=query_spec,
            scratch_shapes=[
                pltpu.VMEM((1, tile_rows, 1), jnp.float32),
                pltpu.VMEM((1, tile_rows, 1), jnp.float32),
                pltpu.VMEM((1, tile_rows, HD), jnp.float32),
            ],
        ),
        out_shape=jax.ShapeDtypeStruct((kv_heads, rows_total, HD), jnp.bfloat16),
    )(table, query_rows, row_group, all_prefix, all_prefix, *state)
    context = jnp.transpose(
        context.reshape(kv_heads, token_rows, repeat_count, HD), (1, 0, 2, 3)
    ).reshape(token_rows, query_heads * HD)
    mixture = jnp.dot(context, w_out, preferred_element_type=jnp.float32)
    mp_devices = lax.axis_size("mp")
    own_columns = lax.dynamic_slice_in_dim(activations, mp_index * part_width, part_width, 1)
    if mp_devices == 2:
        kept = lax.dynamic_slice_in_dim(mixture, mp_index * part_width, part_width, 1)
        sent = lax.dynamic_slice_in_dim(mixture, (1 - mp_index) * part_width, part_width, 1)
        received = lax.ppermute(sent.astype(jnp.bfloat16), "mp", [(0, 1), (1, 0)])
        hidden = (own_columns + (kept + received.astype(jnp.float32))).astype(jnp.bfloat16)
    else:
        mixture = lax.psum_scatter(
            mixture.astype(jnp.bfloat16), "mp", scatter_dimension=1, tiled=True
        ).astype(jnp.float32)
        hidden = (own_columns + mixture).astype(jnp.bfloat16)
    local_last = request_end - 1 - seq_index * token_rows
    onehot = (local_last[:, None] == jnp.arange(token_rows, dtype=jnp.int32)[None, :]).astype(
        jnp.bfloat16
    )
    last_part = jnp.dot(onehot, hidden, preferred_element_type=jnp.float32).astype(jnp.bfloat16)
    summed = butterfly(last_part, "seq", jnp.add)
    if summed is None:
        summed = lax.psum(last_part, "seq")
    last_rows = lax.all_gather(summed, "mp", axis=1, tiled=True).astype(jnp.float32)
    inv_rms = lax.rsqrt(jnp.mean(last_rows * last_rows, -1, keepdims=True) + epsilon)
    last_normed = (last_rows * final_gain.astype(jnp.float32) * inv_rms).astype(jnp.bfloat16)
    logits = jnp.dot(last_normed, w_head, preferred_element_type=jnp.float32)
    local_best = jnp.max(logits, -1)
    best_seq = butterfly(local_best, "seq", jnp.maximum)
    best_all = None if best_seq is None else butterfly(best_seq, "mp", jnp.maximum)
    greatest = lax.pmax(local_best, ("seq", "mp")) if best_all is None else best_all
    return (hidden, suffix_cache, last_normed, greatest)


def solution(mesh):
    return jax.shard_map(
        per_device,
        mesh=mesh,
        in_specs=(
            P("seq", None),
            P(),
            P(None, "seq", None),
            P(),
            P(None, "mp"),
            P(),
            P("mp", None),
            P(),
            P(None, ("seq", "mp")),
        ),
        out_specs=(P("seq", "mp"), P("seq", None), P(), P()),
        check_vma=False,
    )
```

```python
import functools
import math

import jax
import jax.numpy as jnp
from jax import lax
from jax.experimental import pallas as pl
from jax.experimental.pallas import tpu as pltpu
from jax.sharding import PartitionSpec as P

QH = 32
KVH = 4
HD = 64
G = 4
RPG = 8
P_SIZE = 2048
MOST = 1024
PREFIX_CHUNK = 512
SUFFIX_CHUNK = 256
TILE_TOKENS = 32


epsilon = 1e-05


def rotate(source, places, head_count):
    half_dim = HD // 2
    row_count = source.shape[0]
    reshaped = source.reshape(row_count, head_count, HD)
    frequency = 10000.0 ** (-(jnp.arange(half_dim, dtype=jnp.float32) * 2.0 / HD))
    angles = places.astype(jnp.float32)[:, None] * frequency[None, :]
    cos_table = jnp.cos(angles)[:, None, :]
    sine_table = jnp.sin(angles)[:, None, :]
    leading = reshaped[..., :half_dim]
    second = reshaped[..., half_dim:]
    joined = jnp.concatenate(
        [leading * cos_table - second * sine_table, second * cos_table + leading * sine_table], -1
    )
    return joined.reshape(row_count, head_count * HD)


def attend(running, queries, kv_block, allowed):
    old_max, old_sum, numerator = running
    half_width = kv_block.shape[1] // 2
    kv_heads = queries.shape[1]
    key_rows = kv_block[:, :half_width].reshape(kv_block.shape[0], kv_heads, HD)
    val_rows = kv_block[:, half_width:].reshape(kv_block.shape[0], kv_heads, HD)
    scores = jnp.einsum("qgrd,ngd->grqn", queries, key_rows, preferred_element_type=jnp.float32) * (
        1.0 / math.sqrt(HD)
    )
    scores = jnp.where(allowed[None, None], scores, -jnp.inf)
    new_max = jnp.maximum(old_max, jnp.max(scores, -1))
    factor = jnp.exp(old_max - new_max)
    weights = jnp.exp(scores - new_max[..., None])
    new_sum = old_sum * factor + jnp.sum(weights, -1)
    numerator = numerator * factor[..., None] + jnp.einsum(
        "grqn,ngd->grqd", weights.astype(jnp.bfloat16), val_rows, preferred_element_type=jnp.float32
    )
    return (new_max, new_sum, numerator)


def online_update(m_ref, l_ref, acc_ref, head, scores, value, value_contract):
    old_max = m_ref[head]
    new_max = jnp.maximum(old_max, jnp.max(scores, axis=1, keepdims=True))
    factor = jnp.exp(old_max - new_max)
    weights = jnp.exp(scores - new_max)
    l_ref[head] = l_ref[head] * factor + jnp.sum(weights, axis=1, keepdims=True)
    acc_ref[head] = acc_ref[head] * factor + lax.dot_general(
        weights.astype(jnp.bfloat16), value, (((1,), (value_contract,)), ((), ())),
        preferred_element_type=jnp.float32,
    )
    m_ref[head] = new_max


def suffix_kernel(
    table, q_ref, rr_ref, rp_ref, sk_ref, sv_ref, kr_ref, kp_ref, m_ref, l_ref, acc_ref,
    *, kv_heads, suffix_chunk
):
    tile = pl.program_id(0)
    s_lo = table[4 * tile + 2]
    s_hi = table[4 * tile + 3]
    row_request = rr_ref[...]
    row_place = rp_ref[...]
    for head in range(kv_heads):
        query = q_ref[head]
        m_ref[head] = jnp.full(m_ref.shape[1:], -1e30, jnp.float32)
        l_ref[head] = jnp.zeros(l_ref.shape[1:], jnp.float32)
        acc_ref[head] = jnp.zeros(acc_ref.shape[1:], jnp.float32)

        def suffix_step(chunk, carry):
            start = pl.multiple_of(chunk * suffix_chunk, suffix_chunk)
            key = sk_ref[head, pl.ds(start, suffix_chunk), :]
            value = sv_ref[head, pl.ds(start, suffix_chunk), :]
            key_request = kr_ref[pl.ds(chunk, 1), :]
            key_place = kp_ref[pl.ds(chunk, 1), :]
            scores = lax.dot_general(
                query, key, (((1,), (1,)), ((), ())), preferred_element_type=jnp.float32
            ) * (1.0 / math.sqrt(HD))
            allowed = (row_request == key_request) & (key_place <= row_place)
            scores = jnp.where(allowed, scores, -jnp.inf)
            online_update(m_ref, l_ref, acc_ref, head, scores, value, 0)
            return carry

        lax.fori_loop(s_lo, s_hi, suffix_step, 0)


def prefix_kernel(
    table, q_ref, rg_ref, pk_ref, pv_ref, mi_ref, li_ref, ai_ref, o_ref, m_ref, l_ref, acc_ref,
    *, kv_heads, prefix_chunk, parts_per_group
):
    tile = pl.program_id(0)
    p_lo = table[4 * tile]
    p_hi = table[4 * tile + 1]
    row_group = rg_ref[...]
    for head in range(kv_heads):
        query = q_ref[head]
        m_ref[0] = mi_ref[head]
        l_ref[0] = li_ref[head]
        acc_ref[0] = ai_ref[head]

        def prefix_step(group, carry):
            allowed = row_group == group
            for part in range(parts_per_group):
                lanes = slice(part * prefix_chunk, (part + 1) * prefix_chunk)
                key_t = pk_ref[group, head, :, lanes]
                value_t = pv_ref[group, head, :, lanes]
                scores = jnp.dot(query, key_t, preferred_element_type=jnp.float32) * (
                    1.0 / math.sqrt(HD)
                )
                scores = jnp.where(allowed, scores, -jnp.inf)
                online_update(m_ref, l_ref, acc_ref, 0, scores, value_t, 1)
            return carry

        lax.fori_loop(p_lo, p_hi, prefix_step, 0)
        o_ref[head] = (acc_ref[0] / l_ref[0]).astype(o_ref.dtype)


def butterfly(block, axis, combine):
    count = lax.axis_size(axis)
    if count & (count - 1):
        return None
    step = 1
    while step < count:
        partner = lax.ppermute(block, axis, [(i, i ^ step) for i in range(count)])
        block = combine(block, partner)
        step *= 2
    return block


def shifted_back(block, axis, distance):
    count = lax.axis_size(axis)
    route = [(i, i + distance) for i in range(count - distance)]
    return lax.ppermute(block, axis, route)


def per_device(
    tokens, lengths, prefix_cache, attn_gain, w_query, w_keyval, w_out, final_gain, w_head
):
    token_rows = tokens.shape[0]
    model_width = tokens.shape[1]
    seq_devices = lax.axis_size("seq")
    seq_index = lax.axis_index("seq")
    mp_index = lax.axis_index("mp")
    part_width = model_width // lax.axis_size("mp")
    query_heads = w_query.shape[1] // HD
    group_size = QH // KVH
    kv_heads = max(1, query_heads // group_size)
    repeat_count = query_heads // kv_heads
    kv_first = mp_index * query_heads // group_size
    kv_width = KVH * HD
    request_count = lengths.shape[0]
    back_blocks = min(seq_devices - 1, -(-(MOST - 1) // token_rows))

    prefix_rows = prefix_cache.shape[1]
    own_prefix = jnp.concatenate(
        [
            lax.dynamic_slice_in_dim(prefix_cache, kv_first * HD, kv_heads * HD, 2),
            lax.dynamic_slice_in_dim(prefix_cache, kv_width + kv_first * HD, kv_heads * HD, 2),
        ],
        2,
    )
    own_prefix = jnp.transpose(own_prefix.reshape(G, prefix_rows, 2 * kv_heads, HD), (2, 0, 1, 3))
    all_prefix = lax.all_gather(own_prefix, "seq", axis=2, tiled=True)
    prefix_total = seq_devices * prefix_rows
    all_prefix = jnp.transpose(all_prefix, (1, 0, 3, 2))

    activations = tokens.astype(jnp.float32)
    normed = (
        activations
        * lax.rsqrt(jnp.mean(activations * activations, -1, keepdims=True) + epsilon)
        * attn_gain.astype(jnp.float32)
    ).astype(jnp.bfloat16)
    request_end = jnp.cumsum(lengths)
    starts = request_end - lengths
    position = seq_index * token_rows + jnp.arange(token_rows, dtype=jnp.int32)
    request = jnp.sum((position[:, None] >= request_end[None, :]).astype(jnp.int32), 1)
    request_table = request[:, None] == jnp.arange(request_count, dtype=jnp.int32)[None, :]
    offset = position - jnp.sum(jnp.where(request_table, starts[None, :], 0), 1)
    group_of = request // RPG
    keyval = jnp.dot(normed, w_keyval, preferred_element_type=jnp.float32)
    key_rows = rotate(keyval[:, :kv_width], P_SIZE + offset, KVH).astype(jnp.bfloat16)
    val_rows = keyval[:, kv_width:].astype(jnp.bfloat16)
    suffix_cache = jnp.concatenate([key_rows, val_rows], 1)
    own_suffix = jnp.concatenate(
        [
            lax.dynamic_slice_in_dim(key_rows, kv_first * HD, kv_heads * HD, 1),
            lax.dynamic_slice_in_dim(val_rows, kv_first * HD, kv_heads * HD, 1),
        ],
        1,
    )
    own_suffix = jnp.transpose(own_suffix.reshape(token_rows, 2 * kv_heads, HD), (1, 0, 2))
    earlier = [own_suffix] + [
        shifted_back(own_suffix, "seq", distance) for distance in range(1, back_blocks + 1)
    ]

    query_full = jnp.dot(normed, w_query, preferred_element_type=jnp.float32)
    queries = (
        rotate(query_full, P_SIZE + offset, query_heads)
        .astype(jnp.bfloat16)
        .reshape(token_rows, kv_heads, repeat_count, HD)
    )

    window_blocks = back_blocks + 1
    window_rows = window_blocks * token_rows
    window_start = (seq_index - back_blocks) * token_rows
    suffix_window = jnp.concatenate(earlier[::-1], 1)
    suffix_chunk = min(SUFFIX_CHUNK, token_rows)
    prefix_chunk = min(PREFIX_CHUNK, prefix_total)
    chunks_per_group = prefix_total // prefix_chunk
    suffix_chunks = window_rows // suffix_chunk
    key_place = window_start + jnp.arange(window_rows, dtype=jnp.int32)
    key_request = jnp.sum((key_place[:, None] >= request_end[None, :]).astype(jnp.int32), 1)
    key_request = jnp.where(key_place >= 0, key_request, -1)
    key_request = key_request.reshape(suffix_chunks, suffix_chunk)
    key_place = key_place.reshape(suffix_chunks, suffix_chunk)

    tile_tokens = min(TILE_TOKENS, token_rows)
    tile_count = token_rows // tile_tokens
    tile_rows = tile_tokens * repeat_count
    first_token = jnp.arange(tile_count, dtype=jnp.int32) * tile_tokens
    last_token = first_token + tile_tokens - 1
    p_lo = group_of[first_token]
    p_hi = group_of[last_token] + 1
    s_lo = jnp.maximum((starts[request[first_token]] - window_start) // suffix_chunk, 0)
    s_hi = jnp.minimum((position[last_token] - window_start) // suffix_chunk + 1, suffix_chunks)
    table = jnp.stack([p_lo, p_hi, s_lo, s_hi], 1).reshape(-1).astype(jnp.int32)

    query_rows = jnp.transpose(queries, (1, 0, 2, 3)).reshape(
        kv_heads, token_rows * repeat_count, HD
    )
    row_group = jnp.repeat(group_of, repeat_count)[:, None]
    row_request = jnp.repeat(request, repeat_count)[:, None]
    row_place = jnp.repeat(position, repeat_count)[:, None]

    def whole(shape):
        return pl.BlockSpec(shape, lambda tile, table: (0,) * len(shape))

    def half(shape, index):
        return pl.BlockSpec((kv_heads,) + shape[1:], lambda tile, table: (index, 0, 0))

    def prefix_half(index):
        shape = (G, kv_heads, HD, prefix_total)
        return pl.BlockSpec(shape, lambda tile, table: (0, index, 0, 0))

    row_spec = pl.BlockSpec((tile_rows, 1), lambda tile, table: (tile, 0))
    rows_total = token_rows * repeat_count
    state_shapes = [
        jax.ShapeDtypeStruct((kv_heads, rows_total, 1), jnp.float32),
        jax.ShapeDtypeStruct((kv_heads, rows_total, 1), jnp.float32),
        jax.ShapeDtypeStruct((kv_heads, rows_total, HD), jnp.float32),
    ]
    state_specs = [
        pl.BlockSpec((kv_heads, tile_rows, 1), lambda tile, table: (0, tile, 0)),
        pl.BlockSpec((kv_heads, tile_rows, 1), lambda tile, table: (0, tile, 0)),
        pl.BlockSpec((kv_heads, tile_rows, HD), lambda tile, table: (0, tile, 0)),
    ]
    query_spec = pl.BlockSpec((kv_heads, tile_rows, HD), lambda tile, table: (0, tile, 0))
    state = pl.pallas_call(
        functools.partial(suffix_kernel, kv_heads=kv_heads, suffix_chunk=suffix_chunk),
        grid_spec=pltpu.PrefetchScalarGridSpec(
            num_scalar_prefetch=1,
            grid=(tile_count,),
            in_specs=[
                query_spec,
                row_spec,
                row_spec,
                half(suffix_window.shape, 0),
                half(suffix_window.shape, 1),
                whole(key_request.shape),
                whole(key_place.shape),
            ],
            out_specs=state_specs,
        ),
        out_shape=state_shapes,
    )(table, query_rows, row_request, row_place, suffix_window, suffix_window, key_request, key_place)
    context = pl.pallas_call(
        functools.partial(
            prefix_kernel,
            kv_heads=kv_heads,
            prefix_chunk=prefix_chunk,
            parts_per_group=chunks_per_group,
        ),
        grid_spec=pltpu.PrefetchScalarGridSpec(
            num_scalar_prefetch=1,
            grid=(tile_count,),
            in_specs=[query_spec, row_spec, prefix_half(0), prefix_half(1)] + state_specs,
            out_specs=query_spec,
            scratch_shapes=[
                pltpu.VMEM((1, tile_rows, 1), jnp.float32),
                pltpu.VMEM((1, tile_rows, 1), jnp.float32),
                pltpu.VMEM((1, tile_rows, HD), jnp.float32),
            ],
        ),
        out_shape=jax.ShapeDtypeStruct((kv_heads, rows_total, HD), jnp.bfloat16),
    )(table, query_rows, row_group, all_prefix, all_prefix, *state)
    context = jnp.transpose(
        context.reshape(kv_heads, token_rows, repeat_count, HD), (1, 0, 2, 3)
    ).reshape(token_rows, query_heads * HD)
    mixture = jnp.dot(context, w_out, preferred_element_type=jnp.float32)
    mp_devices = lax.axis_size("mp")
    own_columns = lax.dynamic_slice_in_dim(activations, mp_index * part_width, part_width, 1)
    if mp_devices == 2:
        kept = lax.dynamic_slice_in_dim(mixture, mp_index * part_width, part_width, 1)
        sent = lax.dynamic_slice_in_dim(mixture, (1 - mp_index) * part_width, part_width, 1)
        received = lax.ppermute(sent.astype(jnp.bfloat16), "mp", [(0, 1), (1, 0)])
        hidden = (own_columns + (kept + received.astype(jnp.float32))).astype(jnp.bfloat16)
    else:
        mixture = lax.psum_scatter(
            mixture.astype(jnp.bfloat16), "mp", scatter_dimension=1, tiled=True
        ).astype(jnp.float32)
        hidden = (own_columns + mixture).astype(jnp.bfloat16)
    local_last = request_end - 1 - seq_index * token_rows
    onehot = (local_last[:, None] == jnp.arange(token_rows, dtype=jnp.int32)[None, :]).astype(
        jnp.bfloat16
    )
    last_part = jnp.dot(onehot, hidden, preferred_element_type=jnp.float32).astype(jnp.bfloat16)
    summed = butterfly(last_part, "seq", jnp.add)
    if summed is None:
        summed = lax.psum(last_part, "seq")
    last_rows = lax.all_gather(summed, "mp", axis=1, tiled=True).astype(jnp.float32)
    inv_rms = lax.rsqrt(jnp.mean(last_rows * last_rows, -1, keepdims=True) + epsilon)
    last_normed = (last_rows * final_gain.astype(jnp.float32) * inv_rms).astype(jnp.bfloat16)
    logits = jnp.dot(last_normed, w_head, preferred_element_type=jnp.float32)
    local_best = jnp.max(logits, -1)
    best_seq = butterfly(local_best, "seq", jnp.maximum)
    best_all = None if best_seq is None else butterfly(best_seq, "mp", jnp.maximum)
    greatest = lax.pmax(local_best, ("seq", "mp")) if best_all is None else best_all
    return (hidden, suffix_cache, last_normed, greatest)


def solution(mesh):
    return jax.shard_map(
        per_device,
        mesh=mesh,
        in_specs=(
            P("seq", None),
            P(),
            P(None, "seq", None),
            P(),
            P(None, "mp"),
            P(),
            P("mp", None),
            P(),
            P(None, ("seq", "mp")),
        ),
        out_specs=(P("seq", "mp"), P("seq", None), P(), P()),
        check_vma=False,
    )
```

```python
import functools
import math

import jax
import jax.numpy as jnp
from jax import lax
from jax.experimental import pallas as pl
from jax.experimental.pallas import tpu as pltpu
from jax.sharding import PartitionSpec as P

QH = 32
KVH = 4
HD = 64
G = 4
RPG = 8
P_SIZE = 2048
MOST = 1024
PREFIX_CHUNK = 512
SUFFIX_CHUNK = 256
TILE_TOKENS = 128


epsilon = 1e-05


def rotate(source, places, head_count):
    half_dim = HD // 2
    row_count = source.shape[0]
    reshaped = source.reshape(row_count, head_count, HD)
    frequency = 10000.0 ** (-(jnp.arange(half_dim, dtype=jnp.float32) * 2.0 / HD))
    angles = places.astype(jnp.float32)[:, None] * frequency[None, :]
    cos_table = jnp.cos(angles)[:, None, :]
    sine_table = jnp.sin(angles)[:, None, :]
    leading = reshaped[..., :half_dim]
    second = reshaped[..., half_dim:]
    joined = jnp.concatenate(
        [leading * cos_table - second * sine_table, second * cos_table + leading * sine_table], -1
    )
    return joined.reshape(row_count, head_count * HD)


def attend(running, queries, kv_block, allowed):
    old_max, old_sum, numerator = running
    half_width = kv_block.shape[1] // 2
    kv_heads = queries.shape[1]
    key_rows = kv_block[:, :half_width].reshape(kv_block.shape[0], kv_heads, HD)
    val_rows = kv_block[:, half_width:].reshape(kv_block.shape[0], kv_heads, HD)
    scores = jnp.einsum("qgrd,ngd->grqn", queries, key_rows, preferred_element_type=jnp.float32) * (
        1.0 / math.sqrt(HD)
    )
    scores = jnp.where(allowed[None, None], scores, -jnp.inf)
    new_max = jnp.maximum(old_max, jnp.max(scores, -1))
    factor = jnp.exp(old_max - new_max)
    weights = jnp.exp(scores - new_max[..., None])
    new_sum = old_sum * factor + jnp.sum(weights, -1)
    numerator = numerator * factor[..., None] + jnp.einsum(
        "grqn,ngd->grqd", weights.astype(jnp.bfloat16), val_rows, preferred_element_type=jnp.float32
    )
    return (new_max, new_sum, numerator)


def online_update(m_ref, l_ref, acc_ref, head, scores, value, value_contract):
    old_max = m_ref[head]
    new_max = jnp.maximum(old_max, jnp.max(scores, axis=1, keepdims=True))
    factor = jnp.exp(old_max - new_max)
    weights = jnp.exp(scores - new_max)
    l_ref[head] = l_ref[head] * factor + jnp.sum(weights, axis=1, keepdims=True)
    acc_ref[head] = acc_ref[head] * factor + lax.dot_general(
        weights.astype(jnp.bfloat16), value, (((1,), (value_contract,)), ((), ())),
        preferred_element_type=jnp.float32,
    )
    m_ref[head] = new_max


def suffix_kernel(
    table, q_ref, rr_ref, rp_ref, sk_ref, sv_ref, kr_ref, kp_ref, m_ref, l_ref, acc_ref,
    *, kv_heads, suffix_chunk
):
    tile = pl.program_id(0)
    s_lo = table[4 * tile + 2]
    s_hi = table[4 * tile + 3]
    row_request = rr_ref[...]
    row_place = rp_ref[...]
    for head in range(kv_heads):
        query = q_ref[head]
        m_ref[head] = jnp.full(m_ref.shape[1:], -1e30, jnp.float32)
        l_ref[head] = jnp.zeros(l_ref.shape[1:], jnp.float32)
        acc_ref[head] = jnp.zeros(acc_ref.shape[1:], jnp.float32)

        def suffix_step(chunk, carry):
            start = pl.multiple_of(chunk * suffix_chunk, suffix_chunk)
            key = sk_ref[head, pl.ds(start, suffix_chunk), :]
            value = sv_ref[head, pl.ds(start, suffix_chunk), :]
            key_request = kr_ref[pl.ds(chunk, 1), :]
            key_place = kp_ref[pl.ds(chunk, 1), :]
            scores = lax.dot_general(
                query, key, (((1,), (1,)), ((), ())), preferred_element_type=jnp.float32
            ) * (1.0 / math.sqrt(HD))
            allowed = (row_request == key_request) & (key_place <= row_place)
            scores = jnp.where(allowed, scores, -jnp.inf)
            online_update(m_ref, l_ref, acc_ref, head, scores, value, 0)
            return carry

        lax.fori_loop(s_lo, s_hi, suffix_step, 0)


def prefix_kernel(
    table, q_ref, rg_ref, pk_ref, pv_ref, mi_ref, li_ref, ai_ref, o_ref, m_ref, l_ref, acc_ref,
    *, kv_heads, prefix_chunk, parts_per_group
):
    tile = pl.program_id(0)
    p_lo = table[4 * tile]
    p_hi = table[4 * tile + 1]
    row_group = rg_ref[...]
    for head in range(kv_heads):
        query = q_ref[head]
        m_ref[0] = mi_ref[head]
        l_ref[0] = li_ref[head]
        acc_ref[0] = ai_ref[head]

        def prefix_step(group, carry):
            allowed = row_group == group
            for part in range(parts_per_group):
                lanes = slice(part * prefix_chunk, (part + 1) * prefix_chunk)
                key_t = pk_ref[group, head, :, lanes]
                value_t = pv_ref[group, head, :, lanes]
                scores = jnp.dot(query, key_t, preferred_element_type=jnp.float32) * (
                    1.0 / math.sqrt(HD)
                )
                scores = jnp.where(allowed, scores, -jnp.inf)
                online_update(m_ref, l_ref, acc_ref, 0, scores, value_t, 1)
            return carry

        lax.fori_loop(p_lo, p_hi, prefix_step, 0)
        o_ref[head] = (acc_ref[0] / l_ref[0]).astype(o_ref.dtype)


def butterfly(block, axis, combine):
    count = lax.axis_size(axis)
    if count & (count - 1):
        return None
    step = 1
    while step < count:
        partner = lax.ppermute(block, axis, [(i, i ^ step) for i in range(count)])
        block = combine(block, partner)
        step *= 2
    return block


def shifted_back(block, axis, distance):
    count = lax.axis_size(axis)
    route = [(i, i + distance) for i in range(count - distance)]
    return lax.ppermute(block, axis, route)


def per_device(
    tokens, lengths, prefix_cache, attn_gain, w_query, w_keyval, w_out, final_gain, w_head
):
    token_rows = tokens.shape[0]
    model_width = tokens.shape[1]
    seq_devices = lax.axis_size("seq")
    seq_index = lax.axis_index("seq")
    mp_index = lax.axis_index("mp")
    part_width = model_width // lax.axis_size("mp")
    query_heads = w_query.shape[1] // HD
    group_size = QH // KVH
    kv_heads = max(1, query_heads // group_size)
    repeat_count = query_heads // kv_heads
    kv_first = mp_index * query_heads // group_size
    kv_width = KVH * HD
    request_count = lengths.shape[0]
    back_blocks = min(seq_devices - 1, -(-(MOST - 1) // token_rows))

    prefix_rows = prefix_cache.shape[1]
    own_prefix = jnp.concatenate(
        [
            lax.dynamic_slice_in_dim(prefix_cache, kv_first * HD, kv_heads * HD, 2),
            lax.dynamic_slice_in_dim(prefix_cache, kv_width + kv_first * HD, kv_heads * HD, 2),
        ],
        2,
    )
    own_prefix = jnp.transpose(own_prefix.reshape(G, prefix_rows, 2 * kv_heads, HD), (2, 0, 1, 3))
    all_prefix = lax.all_gather(own_prefix, "seq", axis=2, tiled=True)
    prefix_total = seq_devices * prefix_rows
    all_prefix = jnp.transpose(all_prefix, (1, 0, 3, 2))

    activations = tokens.astype(jnp.float32)
    normed = (
        activations
        * lax.rsqrt(jnp.mean(activations * activations, -1, keepdims=True) + epsilon)
        * attn_gain.astype(jnp.float32)
    ).astype(jnp.bfloat16)
    request_end = jnp.cumsum(lengths)
    starts = request_end - lengths
    position = seq_index * token_rows + jnp.arange(token_rows, dtype=jnp.int32)
    request = jnp.sum((position[:, None] >= request_end[None, :]).astype(jnp.int32), 1)
    request_table = request[:, None] == jnp.arange(request_count, dtype=jnp.int32)[None, :]
    offset = position - jnp.sum(jnp.where(request_table, starts[None, :], 0), 1)
    group_of = request // RPG
    keyval = jnp.dot(normed, w_keyval, preferred_element_type=jnp.float32)
    key_rows = rotate(keyval[:, :kv_width], P_SIZE + offset, KVH).astype(jnp.bfloat16)
    val_rows = keyval[:, kv_width:].astype(jnp.bfloat16)
    suffix_cache = jnp.concatenate([key_rows, val_rows], 1)
    own_suffix = jnp.concatenate(
        [
            lax.dynamic_slice_in_dim(key_rows, kv_first * HD, kv_heads * HD, 1),
            lax.dynamic_slice_in_dim(val_rows, kv_first * HD, kv_heads * HD, 1),
        ],
        1,
    )
    own_suffix = jnp.transpose(own_suffix.reshape(token_rows, 2 * kv_heads, HD), (1, 0, 2))
    earlier = [own_suffix] + [
        shifted_back(own_suffix, "seq", distance) for distance in range(1, back_blocks + 1)
    ]

    query_full = jnp.dot(normed, w_query, preferred_element_type=jnp.float32)
    queries = (
        rotate(query_full, P_SIZE + offset, query_heads)
        .astype(jnp.bfloat16)
        .reshape(token_rows, kv_heads, repeat_count, HD)
    )

    window_blocks = back_blocks + 1
    window_rows = window_blocks * token_rows
    window_start = (seq_index - back_blocks) * token_rows
    suffix_window = jnp.concatenate(earlier[::-1], 1)
    suffix_chunk = min(SUFFIX_CHUNK, token_rows)
    prefix_chunk = min(PREFIX_CHUNK, prefix_total)
    chunks_per_group = prefix_total // prefix_chunk
    suffix_chunks = window_rows // suffix_chunk
    key_place = window_start + jnp.arange(window_rows, dtype=jnp.int32)
    key_request = jnp.sum((key_place[:, None] >= request_end[None, :]).astype(jnp.int32), 1)
    key_request = jnp.where(key_place >= 0, key_request, -1)
    key_request = key_request.reshape(suffix_chunks, suffix_chunk)
    key_place = key_place.reshape(suffix_chunks, suffix_chunk)

    tile_tokens = min(TILE_TOKENS, token_rows)
    tile_count = token_rows // tile_tokens
    tile_rows = tile_tokens * repeat_count
    first_token = jnp.arange(tile_count, dtype=jnp.int32) * tile_tokens
    last_token = first_token + tile_tokens - 1
    p_lo = group_of[first_token]
    p_hi = group_of[last_token] + 1
    s_lo = jnp.maximum((starts[request[first_token]] - window_start) // suffix_chunk, 0)
    s_hi = jnp.minimum((position[last_token] - window_start) // suffix_chunk + 1, suffix_chunks)
    table = jnp.stack([p_lo, p_hi, s_lo, s_hi], 1).reshape(-1).astype(jnp.int32)

    query_rows = jnp.transpose(queries, (1, 0, 2, 3)).reshape(
        kv_heads, token_rows * repeat_count, HD
    )
    row_group = jnp.repeat(group_of, repeat_count)[:, None]
    row_request = jnp.repeat(request, repeat_count)[:, None]
    row_place = jnp.repeat(position, repeat_count)[:, None]

    def whole(shape):
        return pl.BlockSpec(shape, lambda tile, table: (0,) * len(shape))

    def half(shape, index):
        return pl.BlockSpec((kv_heads,) + shape[1:], lambda tile, table: (index, 0, 0))

    def prefix_half(index):
        shape = (G, kv_heads, HD, prefix_total)
        return pl.BlockSpec(shape, lambda tile, table: (0, index, 0, 0))

    row_spec = pl.BlockSpec((tile_rows, 1), lambda tile, table: (tile, 0))
    rows_total = token_rows * repeat_count
    state_shapes = [
        jax.ShapeDtypeStruct((kv_heads, rows_total, 1), jnp.float32),
        jax.ShapeDtypeStruct((kv_heads, rows_total, 1), jnp.float32),
        jax.ShapeDtypeStruct((kv_heads, rows_total, HD), jnp.float32),
    ]
    state_specs = [
        pl.BlockSpec((kv_heads, tile_rows, 1), lambda tile, table: (0, tile, 0)),
        pl.BlockSpec((kv_heads, tile_rows, 1), lambda tile, table: (0, tile, 0)),
        pl.BlockSpec((kv_heads, tile_rows, HD), lambda tile, table: (0, tile, 0)),
    ]
    query_spec = pl.BlockSpec((kv_heads, tile_rows, HD), lambda tile, table: (0, tile, 0))
    state = pl.pallas_call(
        functools.partial(suffix_kernel, kv_heads=kv_heads, suffix_chunk=suffix_chunk),
        grid_spec=pltpu.PrefetchScalarGridSpec(
            num_scalar_prefetch=1,
            grid=(tile_count,),
            in_specs=[
                query_spec,
                row_spec,
                row_spec,
                half(suffix_window.shape, 0),
                half(suffix_window.shape, 1),
                whole(key_request.shape),
                whole(key_place.shape),
            ],
            out_specs=state_specs,
        ),
        out_shape=state_shapes,
    )(table, query_rows, row_request, row_place, suffix_window, suffix_window, key_request, key_place)
    context = pl.pallas_call(
        functools.partial(
            prefix_kernel,
            kv_heads=kv_heads,
            prefix_chunk=prefix_chunk,
            parts_per_group=chunks_per_group,
        ),
        grid_spec=pltpu.PrefetchScalarGridSpec(
            num_scalar_prefetch=1,
            grid=(tile_count,),
            in_specs=[query_spec, row_spec, prefix_half(0), prefix_half(1)] + state_specs,
            out_specs=query_spec,
            scratch_shapes=[
                pltpu.VMEM((1, tile_rows, 1), jnp.float32),
                pltpu.VMEM((1, tile_rows, 1), jnp.float32),
                pltpu.VMEM((1, tile_rows, HD), jnp.float32),
            ],
        ),
        out_shape=jax.ShapeDtypeStruct((kv_heads, rows_total, HD), jnp.bfloat16),
    )(table, query_rows, row_group, all_prefix, all_prefix, *state)
    context = jnp.transpose(
        context.reshape(kv_heads, token_rows, repeat_count, HD), (1, 0, 2, 3)
    ).reshape(token_rows, query_heads * HD)
    mixture = jnp.dot(context, w_out, preferred_element_type=jnp.float32)
    mp_devices = lax.axis_size("mp")
    own_columns = lax.dynamic_slice_in_dim(activations, mp_index * part_width, part_width, 1)
    if mp_devices == 2:
        kept = lax.dynamic_slice_in_dim(mixture, mp_index * part_width, part_width, 1)
        sent = lax.dynamic_slice_in_dim(mixture, (1 - mp_index) * part_width, part_width, 1)
        received = lax.ppermute(sent.astype(jnp.bfloat16), "mp", [(0, 1), (1, 0)])
        hidden = (own_columns + (kept + received.astype(jnp.float32))).astype(jnp.bfloat16)
    else:
        mixture = lax.psum_scatter(
            mixture.astype(jnp.bfloat16), "mp", scatter_dimension=1, tiled=True
        ).astype(jnp.float32)
        hidden = (own_columns + mixture).astype(jnp.bfloat16)
    local_last = request_end - 1 - seq_index * token_rows
    onehot = (local_last[:, None] == jnp.arange(token_rows, dtype=jnp.int32)[None, :]).astype(
        jnp.bfloat16
    )
    context_last = jnp.dot(onehot, context, preferred_element_type=jnp.float32)
    mixture_last = jnp.dot(
        context_last.astype(jnp.bfloat16), w_out, preferred_element_type=jnp.float32
    )
    columns_last = jnp.dot(onehot, own_columns.astype(jnp.bfloat16), preferred_element_type=jnp.float32)
    if mp_devices == 2:
        kept = lax.dynamic_slice_in_dim(mixture_last, mp_index * part_width, part_width, 1)
        sent = lax.dynamic_slice_in_dim(mixture_last, (1 - mp_index) * part_width, part_width, 1)
        received = lax.ppermute(sent.astype(jnp.bfloat16), "mp", [(0, 1), (1, 0)])
        last_part = (columns_last + (kept + received.astype(jnp.float32))).astype(jnp.bfloat16)
    else:
        last_part = jnp.dot(onehot, hidden, preferred_element_type=jnp.float32).astype(jnp.bfloat16)
    summed = butterfly(last_part, "seq", jnp.add)
    if summed is None:
        summed = lax.psum(last_part, "seq")
    last_rows = lax.all_gather(summed, "mp", axis=1, tiled=True).astype(jnp.float32)
    inv_rms = lax.rsqrt(jnp.mean(last_rows * last_rows, -1, keepdims=True) + epsilon)
    last_normed = (last_rows * final_gain.astype(jnp.float32) * inv_rms).astype(jnp.bfloat16)
    logits = jnp.dot(last_normed, w_head, preferred_element_type=jnp.float32)
    local_best = jnp.max(logits, -1)
    best_seq = butterfly(local_best, "seq", jnp.maximum)
    best_all = None if best_seq is None else butterfly(best_seq, "mp", jnp.maximum)
    greatest = lax.pmax(local_best, ("seq", "mp")) if best_all is None else best_all
    return (hidden, suffix_cache, last_normed, greatest)


def solution(mesh):
    return jax.shard_map(
        per_device,
        mesh=mesh,
        in_specs=(
            P("seq", None),
            P(),
            P(None, "seq", None),
            P(),
            P(None, "mp"),
            P(),
            P("mp", None),
            P(),
            P(None, ("seq", "mp")),
        ),
        out_specs=(P("seq", "mp"), P("seq", None), P(), P()),
        check_vma=False,
    )
```

```python
import functools
import math

import jax
import jax.numpy as jnp
from jax import lax
from jax.experimental import pallas as pl
from jax.experimental.pallas import tpu as pltpu
from jax.sharding import PartitionSpec as P

QH = 32
KVH = 4
HD = 64
G = 4
RPG = 8
P_SIZE = 2048
MOST = 1024
PREFIX_CHUNK = 512
SUFFIX_CHUNK = 256
TILE_TOKENS = 128


epsilon = 1e-05


def rotate(source, places, head_count):
    half_dim = HD // 2
    row_count = source.shape[0]
    reshaped = source.reshape(row_count, head_count, HD)
    frequency = 10000.0 ** (-(jnp.arange(half_dim, dtype=jnp.float32) * 2.0 / HD))
    angles = places.astype(jnp.float32)[:, None] * frequency[None, :]
    cos_table = jnp.cos(angles)[:, None, :]
    sine_table = jnp.sin(angles)[:, None, :]
    leading = reshaped[..., :half_dim]
    second = reshaped[..., half_dim:]
    joined = jnp.concatenate(
        [leading * cos_table - second * sine_table, second * cos_table + leading * sine_table], -1
    )
    return joined.reshape(row_count, head_count * HD)


def attend(running, queries, kv_block, allowed):
    old_max, old_sum, numerator = running
    half_width = kv_block.shape[1] // 2
    kv_heads = queries.shape[1]
    key_rows = kv_block[:, :half_width].reshape(kv_block.shape[0], kv_heads, HD)
    val_rows = kv_block[:, half_width:].reshape(kv_block.shape[0], kv_heads, HD)
    scores = jnp.einsum("qgrd,ngd->grqn", queries, key_rows, preferred_element_type=jnp.float32) * (
        1.0 / math.sqrt(HD)
    )
    scores = jnp.where(allowed[None, None], scores, -jnp.inf)
    new_max = jnp.maximum(old_max, jnp.max(scores, -1))
    factor = jnp.exp(old_max - new_max)
    weights = jnp.exp(scores - new_max[..., None])
    new_sum = old_sum * factor + jnp.sum(weights, -1)
    numerator = numerator * factor[..., None] + jnp.einsum(
        "grqn,ngd->grqd", weights.astype(jnp.bfloat16), val_rows, preferred_element_type=jnp.float32
    )
    return (new_max, new_sum, numerator)


def online_update(m_ref, l_ref, acc_ref, head, scores, value, value_contract):
    old_max = m_ref[head]
    new_max = jnp.maximum(old_max, jnp.max(scores, axis=1, keepdims=True))
    factor = jnp.exp(old_max - new_max)
    weights = jnp.exp(scores - new_max)
    l_ref[head] = l_ref[head] * factor + jnp.sum(weights, axis=1, keepdims=True)
    acc_ref[head] = acc_ref[head] * factor + lax.dot_general(
        weights.astype(jnp.bfloat16), value, (((1,), (value_contract,)), ((), ())),
        preferred_element_type=jnp.float32,
    )
    m_ref[head] = new_max


def suffix_kernel(
    table, q_ref, rr_ref, rp_ref, sk_ref, sv_ref, kr_ref, kp_ref, m_ref, l_ref, acc_ref,
    *, kv_heads, suffix_chunk
):
    tile = pl.program_id(0)
    s_lo = table[4 * tile + 2]
    s_hi = table[4 * tile + 3]
    row_request = rr_ref[...]
    row_place = rp_ref[...]
    for head in range(kv_heads):
        query = q_ref[head]
        m_ref[head] = jnp.full(m_ref.shape[1:], -1e30, jnp.float32)
        l_ref[head] = jnp.zeros(l_ref.shape[1:], jnp.float32)
        acc_ref[head] = jnp.zeros(acc_ref.shape[1:], jnp.float32)

        def suffix_step(chunk, carry):
            start = pl.multiple_of(chunk * suffix_chunk, suffix_chunk)
            key = sk_ref[head, pl.ds(start, suffix_chunk), :]
            value = sv_ref[head, pl.ds(start, suffix_chunk), :]
            key_request = kr_ref[pl.ds(chunk, 1), :]
            key_place = kp_ref[pl.ds(chunk, 1), :]
            scores = lax.dot_general(
                query, key, (((1,), (1,)), ((), ())), preferred_element_type=jnp.float32
            ) * (1.0 / math.sqrt(HD))
            allowed = (row_request == key_request) & (key_place <= row_place)
            scores = jnp.where(allowed, scores, -jnp.inf)
            online_update(m_ref, l_ref, acc_ref, head, scores, value, 0)
            return carry

        lax.fori_loop(s_lo, s_hi, suffix_step, 0)


def prefix_kernel(
    table, q_ref, rg_ref, pk_ref, pv_ref, mi_ref, li_ref, ai_ref, o_ref, m_ref, l_ref, acc_ref,
    *, kv_heads, prefix_chunk, parts_per_group
):
    tile = pl.program_id(0)
    p_lo = table[4 * tile]
    p_hi = table[4 * tile + 1]
    row_group = rg_ref[...]
    for head in range(kv_heads):
        query = q_ref[head]
        m_ref[0] = mi_ref[head]
        l_ref[0] = li_ref[head]
        acc_ref[0] = ai_ref[head]

        def prefix_step(group, carry):
            allowed = row_group == group
            for part in range(parts_per_group):
                lanes = slice(part * prefix_chunk, (part + 1) * prefix_chunk)
                key_t = pk_ref[group, head, :, lanes]
                value_t = pv_ref[group, head, :, lanes]
                scores = jnp.dot(query, key_t, preferred_element_type=jnp.float32) * (
                    1.0 / math.sqrt(HD)
                )
                scores = jnp.where(allowed, scores, -jnp.inf)
                online_update(m_ref, l_ref, acc_ref, 0, scores, value_t, 1)
            return carry

        lax.fori_loop(p_lo, p_hi, prefix_step, 0)
        o_ref[head] = (acc_ref[0] / l_ref[0]).astype(o_ref.dtype)


def butterfly(block, axis, combine):
    count = lax.axis_size(axis)
    if count & (count - 1):
        return None
    step = 1
    while step < count:
        partner = lax.ppermute(block, axis, [(i, i ^ step) for i in range(count)])
        block = combine(block, partner)
        step *= 2
    return block


def shifted_back(block, axis, distance):
    count = lax.axis_size(axis)
    route = [(i, i + distance) for i in range(count - distance)]
    return lax.ppermute(block, axis, route)


def per_device(
    tokens, lengths, prefix_cache, attn_gain, w_query, w_keyval, w_out, final_gain, w_head
):
    token_rows = tokens.shape[0]
    model_width = tokens.shape[1]
    seq_devices = lax.axis_size("seq")
    seq_index = lax.axis_index("seq")
    mp_index = lax.axis_index("mp")
    part_width = model_width // lax.axis_size("mp")
    query_heads = w_query.shape[1] // HD
    group_size = QH // KVH
    kv_heads = max(1, query_heads // group_size)
    repeat_count = query_heads // kv_heads
    kv_first = mp_index * query_heads // group_size
    kv_width = KVH * HD
    request_count = lengths.shape[0]
    back_blocks = min(seq_devices - 1, -(-(MOST - 1) // token_rows))

    prefix_rows = prefix_cache.shape[1]
    own_prefix = jnp.concatenate(
        [
            lax.dynamic_slice_in_dim(prefix_cache, kv_first * HD, kv_heads * HD, 2),
            lax.dynamic_slice_in_dim(prefix_cache, kv_width + kv_first * HD, kv_heads * HD, 2),
        ],
        2,
    )
    own_prefix = jnp.transpose(own_prefix.reshape(G, prefix_rows, 2 * kv_heads, HD), (0, 2, 3, 1))
    prefix_pieces = [own_prefix] + [
        lax.ppermute(
            own_prefix, "seq", [(i, (i + distance) % seq_devices) for i in range(seq_devices)]
        )
        for distance in range(1, seq_devices)
    ]
    all_prefix = jnp.concatenate(prefix_pieces, 3)
    prefix_total = seq_devices * prefix_rows

    activations = tokens.astype(jnp.float32)
    normed = (
        activations
        * lax.rsqrt(jnp.mean(activations * activations, -1, keepdims=True) + epsilon)
        * attn_gain.astype(jnp.float32)
    ).astype(jnp.bfloat16)
    request_end = jnp.cumsum(lengths)
    starts = request_end - lengths
    position = seq_index * token_rows + jnp.arange(token_rows, dtype=jnp.int32)
    request = jnp.sum((position[:, None] >= request_end[None, :]).astype(jnp.int32), 1)
    request_table = request[:, None] == jnp.arange(request_count, dtype=jnp.int32)[None, :]
    offset = position - jnp.sum(jnp.where(request_table, starts[None, :], 0), 1)
    group_of = request // RPG
    keyval = jnp.dot(normed, w_keyval, preferred_element_type=jnp.float32)
    key_rows = rotate(keyval[:, :kv_width], P_SIZE + offset, KVH).astype(jnp.bfloat16)
    val_rows = keyval[:, kv_width:].astype(jnp.bfloat16)
    suffix_cache = jnp.concatenate([key_rows, val_rows], 1)
    own_suffix = jnp.concatenate(
        [
            lax.dynamic_slice_in_dim(key_rows, kv_first * HD, kv_heads * HD, 1),
            lax.dynamic_slice_in_dim(val_rows, kv_first * HD, kv_heads * HD, 1),
        ],
        1,
    )
    own_suffix = jnp.transpose(own_suffix.reshape(token_rows, 2 * kv_heads, HD), (1, 0, 2))
    earlier = [own_suffix] + [
        shifted_back(own_suffix, "seq", distance) for distance in range(1, back_blocks + 1)
    ]

    query_full = jnp.dot(normed, w_query, preferred_element_type=jnp.float32)
    queries = (
        rotate(query_full, P_SIZE + offset, query_heads)
        .astype(jnp.bfloat16)
        .reshape(token_rows, kv_heads, repeat_count, HD)
    )

    window_blocks = back_blocks + 1
    window_rows = window_blocks * token_rows
    window_start = (seq_index - back_blocks) * token_rows
    suffix_window = jnp.concatenate(earlier[::-1], 1)
    suffix_chunk = min(SUFFIX_CHUNK, token_rows)
    prefix_chunk = min(PREFIX_CHUNK, prefix_total)
    chunks_per_group = prefix_total // prefix_chunk
    suffix_chunks = window_rows // suffix_chunk
    key_place = window_start + jnp.arange(window_rows, dtype=jnp.int32)
    key_request = jnp.sum((key_place[:, None] >= request_end[None, :]).astype(jnp.int32), 1)
    key_request = jnp.where(key_place >= 0, key_request, -1)
    key_request = key_request.reshape(suffix_chunks, suffix_chunk)
    key_place = key_place.reshape(suffix_chunks, suffix_chunk)

    tile_tokens = min(TILE_TOKENS, token_rows)
    tile_count = token_rows // tile_tokens
    tile_rows = tile_tokens * repeat_count
    first_token = jnp.arange(tile_count, dtype=jnp.int32) * tile_tokens
    last_token = first_token + tile_tokens - 1
    p_lo = group_of[first_token]
    p_hi = group_of[last_token] + 1
    s_lo = jnp.maximum((starts[request[first_token]] - window_start) // suffix_chunk, 0)
    s_hi = jnp.minimum((position[last_token] - window_start) // suffix_chunk + 1, suffix_chunks)
    table = jnp.stack([p_lo, p_hi, s_lo, s_hi], 1).reshape(-1).astype(jnp.int32)

    query_rows = jnp.transpose(queries, (1, 0, 2, 3)).reshape(
        kv_heads, token_rows * repeat_count, HD
    )
    row_group = jnp.repeat(group_of, repeat_count)[:, None]
    row_request = jnp.repeat(request, repeat_count)[:, None]
    row_place = jnp.repeat(position, repeat_count)[:, None]

    def whole(shape):
        return pl.BlockSpec(shape, lambda tile, table: (0,) * len(shape))

    def half(shape, index):
        return pl.BlockSpec((kv_heads,) + shape[1:], lambda tile, table: (index, 0, 0))

    def prefix_half(index):
        shape = (G, kv_heads, HD, prefix_total)
        return pl.BlockSpec(shape, lambda tile, table: (0, index, 0, 0))

    row_spec = pl.BlockSpec((tile_rows, 1), lambda tile, table: (tile, 0))
    rows_total = token_rows * repeat_count
    state_shapes = [
        jax.ShapeDtypeStruct((kv_heads, rows_total, 1), jnp.float32),
        jax.ShapeDtypeStruct((kv_heads, rows_total, 1), jnp.float32),
        jax.ShapeDtypeStruct((kv_heads, rows_total, HD), jnp.float32),
    ]
    state_specs = [
        pl.BlockSpec((kv_heads, tile_rows, 1), lambda tile, table: (0, tile, 0)),
        pl.BlockSpec((kv_heads, tile_rows, 1), lambda tile, table: (0, tile, 0)),
        pl.BlockSpec((kv_heads, tile_rows, HD), lambda tile, table: (0, tile, 0)),
    ]
    query_spec = pl.BlockSpec((kv_heads, tile_rows, HD), lambda tile, table: (0, tile, 0))
    state = pl.pallas_call(
        functools.partial(suffix_kernel, kv_heads=kv_heads, suffix_chunk=suffix_chunk),
        grid_spec=pltpu.PrefetchScalarGridSpec(
            num_scalar_prefetch=1,
            grid=(tile_count,),
            in_specs=[
                query_spec,
                row_spec,
                row_spec,
                half(suffix_window.shape, 0),
                half(suffix_window.shape, 1),
                whole(key_request.shape),
                whole(key_place.shape),
            ],
            out_specs=state_specs,
        ),
        out_shape=state_shapes,
    )(table, query_rows, row_request, row_place, suffix_window, suffix_window, key_request, key_place)
    context = pl.pallas_call(
        functools.partial(
            prefix_kernel,
            kv_heads=kv_heads,
            prefix_chunk=prefix_chunk,
            parts_per_group=chunks_per_group,
        ),
        grid_spec=pltpu.PrefetchScalarGridSpec(
            num_scalar_prefetch=1,
            grid=(tile_count,),
            in_specs=[query_spec, row_spec, prefix_half(0), prefix_half(1)] + state_specs,
            out_specs=query_spec,
            scratch_shapes=[
                pltpu.VMEM((1, tile_rows, 1), jnp.float32),
                pltpu.VMEM((1, tile_rows, 1), jnp.float32),
                pltpu.VMEM((1, tile_rows, HD), jnp.float32),
            ],
        ),
        out_shape=jax.ShapeDtypeStruct((kv_heads, rows_total, HD), jnp.bfloat16),
    )(table, query_rows, row_group, all_prefix, all_prefix, *state)
    context = jnp.transpose(
        context.reshape(kv_heads, token_rows, repeat_count, HD), (1, 0, 2, 3)
    ).reshape(token_rows, query_heads * HD)
    mixture = jnp.dot(context, w_out, preferred_element_type=jnp.float32)
    mp_devices = lax.axis_size("mp")
    own_columns = lax.dynamic_slice_in_dim(activations, mp_index * part_width, part_width, 1)
    if mp_devices == 2:
        kept = lax.dynamic_slice_in_dim(mixture, mp_index * part_width, part_width, 1)
        sent = lax.dynamic_slice_in_dim(mixture, (1 - mp_index) * part_width, part_width, 1)
        received = lax.ppermute(sent.astype(jnp.bfloat16), "mp", [(0, 1), (1, 0)])
        hidden = (own_columns + (kept + received.astype(jnp.float32))).astype(jnp.bfloat16)
    else:
        mixture = lax.psum_scatter(
            mixture.astype(jnp.bfloat16), "mp", scatter_dimension=1, tiled=True
        ).astype(jnp.float32)
        hidden = (own_columns + mixture).astype(jnp.bfloat16)
    local_last = request_end - 1 - seq_index * token_rows
    onehot = (local_last[:, None] == jnp.arange(token_rows, dtype=jnp.int32)[None, :]).astype(
        jnp.bfloat16
    )
    last_part = jnp.dot(onehot, hidden, preferred_element_type=jnp.float32).astype(jnp.bfloat16)
    summed = butterfly(last_part, "seq", jnp.add)
    if summed is None:
        summed = lax.psum(last_part, "seq")
    last_rows = lax.all_gather(summed, "mp", axis=1, tiled=True).astype(jnp.float32)
    inv_rms = lax.rsqrt(jnp.mean(last_rows * last_rows, -1, keepdims=True) + epsilon)
    last_normed = (last_rows * final_gain.astype(jnp.float32) * inv_rms).astype(jnp.bfloat16)
    logits = jnp.dot(last_normed, w_head, preferred_element_type=jnp.float32)
    local_best = jnp.max(logits, -1)
    best_seq = butterfly(local_best, "seq", jnp.maximum)
    best_all = None if best_seq is None else butterfly(best_seq, "mp", jnp.maximum)
    greatest = lax.pmax(local_best, ("seq", "mp")) if best_all is None else best_all
    return (hidden, suffix_cache, last_normed, greatest)


def solution(mesh):
    return jax.shard_map(
        per_device,
        mesh=mesh,
        in_specs=(
            P("seq", None),
            P(),
            P(None, "seq", None),
            P(),
            P(None, "mp"),
            P(),
            P("mp", None),
            P(),
            P(None, ("seq", "mp")),
        ),
        out_specs=(P("seq", "mp"), P("seq", None), P(), P()),
        check_vma=False,
    )
```

```python
import functools
import math

import jax
import jax.numpy as jnp
from jax import lax
from jax.experimental import pallas as pl
from jax.experimental.pallas import tpu as pltpu
from jax.sharding import PartitionSpec as P

QH = 32
KVH = 4
HD = 64
G = 4
RPG = 8
P_SIZE = 2048
MOST = 1024
PREFIX_CHUNK = 512
SUFFIX_CHUNK = 256
TILE_TOKENS = 128


epsilon = 1e-05


def rotate(source, places, head_count):
    half_dim = HD // 2
    row_count = source.shape[0]
    reshaped = source.reshape(row_count, head_count, HD)
    frequency = 10000.0 ** (-(jnp.arange(half_dim, dtype=jnp.float32) * 2.0 / HD))
    angles = places.astype(jnp.float32)[:, None] * frequency[None, :]
    cos_table = jnp.cos(angles)[:, None, :]
    sine_table = jnp.sin(angles)[:, None, :]
    leading = reshaped[..., :half_dim]
    second = reshaped[..., half_dim:]
    joined = jnp.concatenate(
        [leading * cos_table - second * sine_table, second * cos_table + leading * sine_table], -1
    )
    return joined.reshape(row_count, head_count * HD)


def attend(running, queries, kv_block, allowed):
    old_max, old_sum, numerator = running
    half_width = kv_block.shape[1] // 2
    kv_heads = queries.shape[1]
    key_rows = kv_block[:, :half_width].reshape(kv_block.shape[0], kv_heads, HD)
    val_rows = kv_block[:, half_width:].reshape(kv_block.shape[0], kv_heads, HD)
    scores = jnp.einsum("qgrd,ngd->grqn", queries, key_rows, preferred_element_type=jnp.float32) * (
        1.0 / math.sqrt(HD)
    )
    scores = jnp.where(allowed[None, None], scores, -jnp.inf)
    new_max = jnp.maximum(old_max, jnp.max(scores, -1))
    factor = jnp.exp(old_max - new_max)
    weights = jnp.exp(scores - new_max[..., None])
    new_sum = old_sum * factor + jnp.sum(weights, -1)
    numerator = numerator * factor[..., None] + jnp.einsum(
        "grqn,ngd->grqd", weights.astype(jnp.bfloat16), val_rows, preferred_element_type=jnp.float32
    )
    return (new_max, new_sum, numerator)


def online_update(m_ref, l_ref, acc_ref, head, scores, value, value_contract):
    old_max = m_ref[head]
    new_max = jnp.maximum(old_max, jnp.max(scores, axis=1, keepdims=True))
    factor = jnp.exp(old_max - new_max)
    weights = jnp.exp(scores - new_max)
    l_ref[head] = l_ref[head] * factor + jnp.sum(weights, axis=1, keepdims=True)
    acc_ref[head] = acc_ref[head] * factor + lax.dot_general(
        weights.astype(jnp.bfloat16), value, (((1,), (value_contract,)), ((), ())),
        preferred_element_type=jnp.float32,
    )
    m_ref[head] = new_max


def suffix_kernel(
    table, q_ref, rr_ref, rp_ref, sk_ref, sv_ref, kr_ref, kp_ref, m_ref, l_ref, acc_ref,
    *, kv_heads, suffix_chunk
):
    tile = pl.program_id(0)
    s_lo = table[4 * tile + 2]
    s_hi = table[4 * tile + 3]
    row_request = rr_ref[...]
    row_place = rp_ref[...]
    for head in range(kv_heads):
        query = q_ref[head]
        m_ref[head] = jnp.full(m_ref.shape[1:], -1e30, jnp.float32)
        l_ref[head] = jnp.zeros(l_ref.shape[1:], jnp.float32)
        acc_ref[head] = jnp.zeros(acc_ref.shape[1:], jnp.float32)

        def suffix_step(chunk, carry):
            start = pl.multiple_of(chunk * suffix_chunk, suffix_chunk)
            key = sk_ref[head, pl.ds(start, suffix_chunk), :]
            value = sv_ref[head, pl.ds(start, suffix_chunk), :]
            key_request = kr_ref[pl.ds(chunk, 1), :]
            key_place = kp_ref[pl.ds(chunk, 1), :]
            scores = lax.dot_general(
                query, key, (((1,), (1,)), ((), ())), preferred_element_type=jnp.float32
            ) * (1.0 / math.sqrt(HD))
            allowed = (row_request == key_request) & (key_place <= row_place)
            scores = jnp.where(allowed, scores, -jnp.inf)
            online_update(m_ref, l_ref, acc_ref, head, scores, value, 0)
            return carry

        lax.fori_loop(s_lo, s_hi, suffix_step, 0)


def prefix_kernel(
    table, q_ref, rg_ref, pk_ref, pv_ref, mi_ref, li_ref, ai_ref, o_ref, m_ref, l_ref, acc_ref,
    *, kv_heads, prefix_chunk, parts_per_group
):
    tile = pl.program_id(0)
    p_lo = table[4 * tile]
    p_hi = table[4 * tile + 1]
    row_group = rg_ref[...]
    for head in range(kv_heads):
        query = q_ref[head]
        m_ref[0] = mi_ref[head]
        l_ref[0] = li_ref[head]
        acc_ref[0] = ai_ref[head]

        def prefix_step(group, carry):
            allowed = row_group == group
            for part in range(parts_per_group):
                lanes = slice(part * prefix_chunk, (part + 1) * prefix_chunk)
                key_t = pk_ref[group, head, :, lanes]
                value_t = pv_ref[group, head, :, lanes]
                scores = jnp.dot(query, key_t, preferred_element_type=jnp.float32) * (
                    1.0 / math.sqrt(HD)
                )
                scores = jnp.where(allowed, scores, -jnp.inf)
                online_update(m_ref, l_ref, acc_ref, 0, scores, value_t, 1)
            return carry

        lax.fori_loop(p_lo, p_hi, prefix_step, 0)
        o_ref[head] = (acc_ref[0] / l_ref[0]).astype(o_ref.dtype)


def butterfly(block, axis, combine):
    count = lax.axis_size(axis)
    if count & (count - 1):
        return None
    step = 1
    while step < count:
        partner = lax.ppermute(block, axis, [(i, i ^ step) for i in range(count)])
        block = combine(block, partner)
        step *= 2
    return block


def shifted_back(block, axis, distance):
    count = lax.axis_size(axis)
    route = [(i, i + distance) for i in range(count - distance)]
    return lax.ppermute(block, axis, route)


def per_device(
    tokens, lengths, prefix_cache, attn_gain, w_query, w_keyval, w_out, final_gain, w_head
):
    token_rows = tokens.shape[0]
    model_width = tokens.shape[1]
    seq_devices = lax.axis_size("seq")
    seq_index = lax.axis_index("seq")
    mp_index = lax.axis_index("mp")
    part_width = model_width // lax.axis_size("mp")
    query_heads = w_query.shape[1] // HD
    group_size = QH // KVH
    kv_heads = max(1, query_heads // group_size)
    repeat_count = query_heads // kv_heads
    kv_first = mp_index * query_heads // group_size
    kv_width = KVH * HD
    request_count = lengths.shape[0]
    back_blocks = min(seq_devices - 1, -(-(MOST - 1) // token_rows))

    prefix_rows = prefix_cache.shape[1]
    own_prefix = jnp.concatenate(
        [
            lax.dynamic_slice_in_dim(prefix_cache, kv_first * HD, kv_heads * HD, 2),
            lax.dynamic_slice_in_dim(prefix_cache, kv_width + kv_first * HD, kv_heads * HD, 2),
        ],
        2,
    )
    own_prefix = jnp.transpose(own_prefix.reshape(G, prefix_rows, 2 * kv_heads, HD), (2, 0, 1, 3))
    all_prefix = lax.all_gather(own_prefix, "seq", axis=2, tiled=True)
    prefix_total = seq_devices * prefix_rows
    all_prefix = jnp.transpose(all_prefix, (1, 0, 3, 2))

    activations = tokens.astype(jnp.float32)
    normed = (
        activations
        * lax.rsqrt(jnp.mean(activations * activations, -1, keepdims=True) + epsilon)
        * attn_gain.astype(jnp.float32)
    ).astype(jnp.bfloat16)
    request_end = jnp.cumsum(lengths)
    starts = request_end - lengths
    position = seq_index * token_rows + jnp.arange(token_rows, dtype=jnp.int32)
    request = jnp.sum((position[:, None] >= request_end[None, :]).astype(jnp.int32), 1)
    request_table = request[:, None] == jnp.arange(request_count, dtype=jnp.int32)[None, :]
    offset = position - jnp.sum(jnp.where(request_table, starts[None, :], 0), 1)
    group_of = request // RPG
    keyval = jnp.dot(normed, w_keyval, preferred_element_type=jnp.float32)
    key_rows = rotate(keyval[:, :kv_width], P_SIZE + offset, KVH).astype(jnp.bfloat16)
    val_rows = keyval[:, kv_width:].astype(jnp.bfloat16)
    suffix_cache = jnp.concatenate([key_rows, val_rows], 1)
    own_suffix = jnp.concatenate(
        [
            lax.dynamic_slice_in_dim(key_rows, kv_first * HD, kv_heads * HD, 1),
            lax.dynamic_slice_in_dim(val_rows, kv_first * HD, kv_heads * HD, 1),
        ],
        1,
    )
    own_suffix = jnp.transpose(own_suffix.reshape(token_rows, 2 * kv_heads, HD), (1, 0, 2))
    earlier = [own_suffix] + [
        shifted_back(own_suffix, "seq", distance) for distance in range(1, back_blocks + 1)
    ]

    query_full = jnp.dot(normed, w_query, preferred_element_type=jnp.float32)
    queries = (
        rotate(query_full, P_SIZE + offset, query_heads)
        .astype(jnp.bfloat16)
        .reshape(token_rows, kv_heads, repeat_count, HD)
    )

    window_blocks = back_blocks + 1
    window_rows = window_blocks * token_rows
    window_start = (seq_index - back_blocks) * token_rows
    suffix_window = jnp.concatenate(earlier[::-1], 1)
    suffix_chunk = min(SUFFIX_CHUNK, token_rows)
    prefix_chunk = min(PREFIX_CHUNK, prefix_total)
    chunks_per_group = prefix_total // prefix_chunk
    suffix_chunks = window_rows // suffix_chunk
    key_place = window_start + jnp.arange(window_rows, dtype=jnp.int32)
    key_request = jnp.sum((key_place[:, None] >= request_end[None, :]).astype(jnp.int32), 1)
    key_request = jnp.where(key_place >= 0, key_request, -1)
    key_request = key_request.reshape(suffix_chunks, suffix_chunk)
    key_place = key_place.reshape(suffix_chunks, suffix_chunk)

    tile_tokens = min(TILE_TOKENS, token_rows)
    tile_count = token_rows // tile_tokens
    tile_rows = tile_tokens * repeat_count
    first_token = jnp.arange(tile_count, dtype=jnp.int32) * tile_tokens
    last_token = first_token + tile_tokens - 1
    p_lo = group_of[first_token]
    p_hi = group_of[last_token] + 1
    s_lo = jnp.maximum((starts[request[first_token]] - window_start) // suffix_chunk, 0)
    s_hi = jnp.minimum((position[last_token] - window_start) // suffix_chunk + 1, suffix_chunks)
    table = jnp.stack([p_lo, p_hi, s_lo, s_hi], 1).reshape(-1).astype(jnp.int32)

    query_rows = jnp.transpose(queries, (1, 0, 2, 3)).reshape(
        kv_heads, token_rows * repeat_count, HD
    )
    row_group = jnp.repeat(group_of, repeat_count)[:, None]
    row_request = jnp.repeat(request, repeat_count)[:, None]
    row_place = jnp.repeat(position, repeat_count)[:, None]

    def whole(shape):
        return pl.BlockSpec(shape, lambda tile, table: (0,) * len(shape))

    def half(shape, index):
        return pl.BlockSpec((kv_heads,) + shape[1:], lambda tile, table: (index, 0, 0))

    def prefix_half(index):
        shape = (G, kv_heads, HD, prefix_total)
        return pl.BlockSpec(shape, lambda tile, table: (0, index, 0, 0))

    row_spec = pl.BlockSpec((tile_rows, 1), lambda tile, table: (tile, 0))
    rows_total = token_rows * repeat_count
    state_shapes = [
        jax.ShapeDtypeStruct((kv_heads, rows_total, 1), jnp.float32),
        jax.ShapeDtypeStruct((kv_heads, rows_total, 1), jnp.float32),
        jax.ShapeDtypeStruct((kv_heads, rows_total, HD), jnp.float32),
    ]
    state_specs = [
        pl.BlockSpec((kv_heads, tile_rows, 1), lambda tile, table: (0, tile, 0)),
        pl.BlockSpec((kv_heads, tile_rows, 1), lambda tile, table: (0, tile, 0)),
        pl.BlockSpec((kv_heads, tile_rows, HD), lambda tile, table: (0, tile, 0)),
    ]
    query_spec = pl.BlockSpec((kv_heads, tile_rows, HD), lambda tile, table: (0, tile, 0))
    state = pl.pallas_call(
        functools.partial(suffix_kernel, kv_heads=kv_heads, suffix_chunk=suffix_chunk),
        grid_spec=pltpu.PrefetchScalarGridSpec(
            num_scalar_prefetch=1,
            grid=(tile_count,),
            in_specs=[
                query_spec,
                row_spec,
                row_spec,
                half(suffix_window.shape, 0),
                half(suffix_window.shape, 1),
                whole(key_request.shape),
                whole(key_place.shape),
            ],
            out_specs=state_specs,
        ),
        out_shape=state_shapes,
    )(table, query_rows, row_request, row_place, suffix_window, suffix_window, key_request, key_place)
    context = pl.pallas_call(
        functools.partial(
            prefix_kernel,
            kv_heads=kv_heads,
            prefix_chunk=prefix_chunk,
            parts_per_group=chunks_per_group,
        ),
        grid_spec=pltpu.PrefetchScalarGridSpec(
            num_scalar_prefetch=1,
            grid=(tile_count,),
            in_specs=[query_spec, row_spec, prefix_half(0), prefix_half(1)] + state_specs,
            out_specs=query_spec,
            scratch_shapes=[
                pltpu.VMEM((1, tile_rows, 1), jnp.float32),
                pltpu.VMEM((1, tile_rows, 1), jnp.float32),
                pltpu.VMEM((1, tile_rows, HD), jnp.float32),
            ],
        ),
        out_shape=jax.ShapeDtypeStruct((kv_heads, rows_total, HD), jnp.bfloat16),
    )(table, query_rows, row_group, all_prefix, all_prefix, *state)
    context = jnp.transpose(
        context.reshape(kv_heads, token_rows, repeat_count, HD), (1, 0, 2, 3)
    ).reshape(token_rows, query_heads * HD)
    mp_devices = lax.axis_size("mp")
    own_columns = lax.dynamic_slice_in_dim(activations, mp_index * part_width, part_width, 1)
    if mp_devices == 2:
        sent = jnp.dot(
            context,
            lax.dynamic_slice_in_dim(w_out, (1 - mp_index) * part_width, part_width, 1),
            preferred_element_type=jnp.float32,
        )
        received = lax.ppermute(sent.astype(jnp.bfloat16), "mp", [(0, 1), (1, 0)])
        kept = jnp.dot(
            context,
            lax.dynamic_slice_in_dim(w_out, mp_index * part_width, part_width, 1),
            preferred_element_type=jnp.float32,
        )
        hidden = (own_columns + (kept + received.astype(jnp.float32))).astype(jnp.bfloat16)
    else:
        mixture = jnp.dot(context, w_out, preferred_element_type=jnp.float32)
        mixture = lax.psum_scatter(
            mixture.astype(jnp.bfloat16), "mp", scatter_dimension=1, tiled=True
        ).astype(jnp.float32)
        hidden = (own_columns + mixture).astype(jnp.bfloat16)
    local_last = request_end - 1 - seq_index * token_rows
    onehot = (local_last[:, None] == jnp.arange(token_rows, dtype=jnp.int32)[None, :]).astype(
        jnp.bfloat16
    )
    last_part = jnp.dot(onehot, hidden, preferred_element_type=jnp.float32).astype(jnp.bfloat16)
    summed = butterfly(last_part, "seq", jnp.add)
    if summed is None:
        summed = lax.psum(last_part, "seq")
    last_rows = lax.all_gather(summed, "mp", axis=1, tiled=True).astype(jnp.float32)
    inv_rms = lax.rsqrt(jnp.mean(last_rows * last_rows, -1, keepdims=True) + epsilon)
    last_normed = (last_rows * final_gain.astype(jnp.float32) * inv_rms).astype(jnp.bfloat16)
    logits = jnp.dot(last_normed, w_head, preferred_element_type=jnp.float32)
    local_best = jnp.max(logits, -1)
    best_seq = butterfly(local_best, "seq", jnp.maximum)
    best_all = None if best_seq is None else butterfly(best_seq, "mp", jnp.maximum)
    greatest = lax.pmax(local_best, ("seq", "mp")) if best_all is None else best_all
    return (hidden, suffix_cache, last_normed, greatest)


def solution(mesh):
    return jax.shard_map(
        per_device,
        mesh=mesh,
        in_specs=(
            P("seq", None),
            P(),
            P(None, "seq", None),
            P(),
            P(None, "mp"),
            P(),
            P("mp", None),
            P(),
            P(None, ("seq", "mp")),
        ),
        out_specs=(P("seq", "mp"), P("seq", None), P(), P()),
        check_vma=False,
    )
```

```python
import functools
import math

import jax
import jax.numpy as jnp
from jax import lax
from jax.experimental import pallas as pl
from jax.experimental.pallas import tpu as pltpu
from jax.sharding import PartitionSpec as P

QH = 32
KVH = 4
HD = 64
G = 4
RPG = 8
P_SIZE = 2048
MOST = 1024
PREFIX_CHUNK = 512
SUFFIX_CHUNK = 256
TILE_TOKENS = 128


epsilon = 1e-05


def rotate(source, places, head_count):
    half_dim = HD // 2
    row_count = source.shape[0]
    reshaped = source.reshape(row_count, head_count, HD)
    frequency = 10000.0 ** (-(jnp.arange(half_dim, dtype=jnp.float32) * 2.0 / HD))
    angles = places.astype(jnp.float32)[:, None] * frequency[None, :]
    cos_table = jnp.cos(angles)[:, None, :]
    sine_table = jnp.sin(angles)[:, None, :]
    leading = reshaped[..., :half_dim]
    second = reshaped[..., half_dim:]
    joined = jnp.concatenate(
        [leading * cos_table - second * sine_table, second * cos_table + leading * sine_table], -1
    )
    return joined.reshape(row_count, head_count * HD)


def attend(running, queries, kv_block, allowed):
    old_max, old_sum, numerator = running
    half_width = kv_block.shape[1] // 2
    kv_heads = queries.shape[1]
    key_rows = kv_block[:, :half_width].reshape(kv_block.shape[0], kv_heads, HD)
    val_rows = kv_block[:, half_width:].reshape(kv_block.shape[0], kv_heads, HD)
    scores = jnp.einsum("qgrd,ngd->grqn", queries, key_rows, preferred_element_type=jnp.float32) * (
        1.0 / math.sqrt(HD)
    )
    scores = jnp.where(allowed[None, None], scores, -jnp.inf)
    new_max = jnp.maximum(old_max, jnp.max(scores, -1))
    factor = jnp.exp(old_max - new_max)
    weights = jnp.exp(scores - new_max[..., None])
    new_sum = old_sum * factor + jnp.sum(weights, -1)
    numerator = numerator * factor[..., None] + jnp.einsum(
        "grqn,ngd->grqd", weights.astype(jnp.bfloat16), val_rows, preferred_element_type=jnp.float32
    )
    return (new_max, new_sum, numerator)


def online_update(m_ref, l_ref, acc_ref, head, scores, value, value_contract):
    old_max = m_ref[head]
    new_max = jnp.maximum(old_max, jnp.max(scores, axis=1, keepdims=True))
    factor = jnp.exp(old_max - new_max)
    weights = jnp.exp(scores - new_max)
    l_ref[head] = l_ref[head] * factor + jnp.sum(weights, axis=1, keepdims=True)
    acc_ref[head] = acc_ref[head] * factor + lax.dot_general(
        weights.astype(jnp.bfloat16), value, (((1,), (value_contract,)), ((), ())),
        preferred_element_type=jnp.float32,
    )
    m_ref[head] = new_max


def suffix_kernel(
    table, q_ref, rr_ref, rp_ref, sk_ref, sv_ref, kr_ref, kp_ref, m_ref, l_ref, acc_ref,
    *, kv_heads, suffix_chunk
):
    tile = pl.program_id(0)
    s_lo = table[4 * tile + 2]
    s_hi = table[4 * tile + 3]
    row_request = rr_ref[...]
    row_place = rp_ref[...]
    for head in range(kv_heads):
        query = q_ref[head]
        m_ref[head] = jnp.full(m_ref.shape[1:], -1e30, jnp.float32)
        l_ref[head] = jnp.zeros(l_ref.shape[1:], jnp.float32)
        acc_ref[head] = jnp.zeros(acc_ref.shape[1:], jnp.float32)

        def suffix_step(chunk, carry):
            start = pl.multiple_of(chunk * suffix_chunk, suffix_chunk)
            key = sk_ref[head, pl.ds(start, suffix_chunk), :]
            value = sv_ref[head, pl.ds(start, suffix_chunk), :]
            key_request = kr_ref[pl.ds(chunk, 1), :]
            key_place = kp_ref[pl.ds(chunk, 1), :]
            scores = lax.dot_general(
                query, key, (((1,), (1,)), ((), ())), preferred_element_type=jnp.float32
            ) * (1.0 / math.sqrt(HD))
            allowed = (row_request == key_request) & (key_place <= row_place)
            scores = jnp.where(allowed, scores, -jnp.inf)
            online_update(m_ref, l_ref, acc_ref, head, scores, value, 0)
            return carry

        lax.fori_loop(s_lo, s_hi, suffix_step, 0)


def prefix_kernel(
    table, q_ref, rg_ref, pk_ref, pv_ref, mi_ref, li_ref, ai_ref, o_ref, m_ref, l_ref, acc_ref,
    *, kv_heads, prefix_chunk, parts_per_group
):
    tile = pl.program_id(0)
    p_lo = table[4 * tile]
    p_hi = table[4 * tile + 1]
    row_group = rg_ref[...]
    for head in range(kv_heads):
        query = q_ref[head]
        m_ref[0] = mi_ref[head]
        l_ref[0] = li_ref[head]
        acc_ref[0] = ai_ref[head]

        def prefix_step(group, carry, masked):
            allowed = row_group == group
            for part in range(parts_per_group):
                lanes = slice(part * prefix_chunk, (part + 1) * prefix_chunk)
                key_t = pk_ref[group, head, :, lanes]
                value_t = pv_ref[group, head, :, lanes]
                scores = jnp.dot(query, key_t, preferred_element_type=jnp.float32) * (
                    1.0 / math.sqrt(HD)
                )
                if masked:
                    scores = jnp.where(allowed, scores, -jnp.inf)
                online_update(m_ref, l_ref, acc_ref, 0, scores, value_t, 1)
            return carry

        @pl.when(p_hi - p_lo == 1)
        def _():
            prefix_step(p_lo, 0, False)

        @pl.when(p_hi - p_lo != 1)
        def _():
            lax.fori_loop(p_lo, p_hi, functools.partial(prefix_step, masked=True), 0)


        o_ref[head] = (acc_ref[0] / l_ref[0]).astype(o_ref.dtype)


def butterfly(block, axis, combine):
    count = lax.axis_size(axis)
    if count & (count - 1):
        return None
    step = 1
    while step < count:
        partner = lax.ppermute(block, axis, [(i, i ^ step) for i in range(count)])
        block = combine(block, partner)
        step *= 2
    return block


def shifted_back(block, axis, distance):
    count = lax.axis_size(axis)
    route = [(i, i + distance) for i in range(count - distance)]
    return lax.ppermute(block, axis, route)


def per_device(
    tokens, lengths, prefix_cache, attn_gain, w_query, w_keyval, w_out, final_gain, w_head
):
    token_rows = tokens.shape[0]
    model_width = tokens.shape[1]
    seq_devices = lax.axis_size("seq")
    seq_index = lax.axis_index("seq")
    mp_index = lax.axis_index("mp")
    part_width = model_width // lax.axis_size("mp")
    query_heads = w_query.shape[1] // HD
    group_size = QH // KVH
    kv_heads = max(1, query_heads // group_size)
    repeat_count = query_heads // kv_heads
    kv_first = mp_index * query_heads // group_size
    kv_width = KVH * HD
    request_count = lengths.shape[0]
    back_blocks = min(seq_devices - 1, -(-(MOST - 1) // token_rows))

    prefix_rows = prefix_cache.shape[1]
    own_prefix = jnp.concatenate(
        [
            lax.dynamic_slice_in_dim(prefix_cache, kv_first * HD, kv_heads * HD, 2),
            lax.dynamic_slice_in_dim(prefix_cache, kv_width + kv_first * HD, kv_heads * HD, 2),
        ],
        2,
    )
    own_prefix = jnp.transpose(own_prefix.reshape(G, prefix_rows, 2 * kv_heads, HD), (2, 0, 1, 3))
    all_prefix = lax.all_gather(own_prefix, "seq", axis=2, tiled=True)
    prefix_total = seq_devices * prefix_rows
    all_prefix = jnp.transpose(all_prefix, (1, 0, 3, 2))

    activations = tokens.astype(jnp.float32)
    normed = (
        activations
        * lax.rsqrt(jnp.mean(activations * activations, -1, keepdims=True) + epsilon)
        * attn_gain.astype(jnp.float32)
    ).astype(jnp.bfloat16)
    request_end = jnp.cumsum(lengths)
    starts = request_end - lengths
    position = seq_index * token_rows + jnp.arange(token_rows, dtype=jnp.int32)
    request = jnp.sum((position[:, None] >= request_end[None, :]).astype(jnp.int32), 1)
    request_table = request[:, None] == jnp.arange(request_count, dtype=jnp.int32)[None, :]
    offset = position - jnp.sum(jnp.where(request_table, starts[None, :], 0), 1)
    group_of = request // RPG
    keyval = jnp.dot(normed, w_keyval, preferred_element_type=jnp.float32)
    key_rows = rotate(keyval[:, :kv_width], P_SIZE + offset, KVH).astype(jnp.bfloat16)
    val_rows = keyval[:, kv_width:].astype(jnp.bfloat16)
    suffix_cache = jnp.concatenate([key_rows, val_rows], 1)
    own_suffix = jnp.concatenate(
        [
            lax.dynamic_slice_in_dim(key_rows, kv_first * HD, kv_heads * HD, 1),
            lax.dynamic_slice_in_dim(val_rows, kv_first * HD, kv_heads * HD, 1),
        ],
        1,
    )
    own_suffix = jnp.transpose(own_suffix.reshape(token_rows, 2 * kv_heads, HD), (1, 0, 2))
    earlier = [own_suffix] + [
        shifted_back(own_suffix, "seq", distance) for distance in range(1, back_blocks + 1)
    ]

    query_full = jnp.dot(normed, w_query, preferred_element_type=jnp.float32)
    queries = (
        rotate(query_full, P_SIZE + offset, query_heads)
        .astype(jnp.bfloat16)
        .reshape(token_rows, kv_heads, repeat_count, HD)
    )

    window_blocks = back_blocks + 1
    window_rows = window_blocks * token_rows
    window_start = (seq_index - back_blocks) * token_rows
    suffix_window = jnp.concatenate(earlier[::-1], 1)
    suffix_chunk = min(SUFFIX_CHUNK, token_rows)
    prefix_chunk = min(PREFIX_CHUNK, prefix_total)
    chunks_per_group = prefix_total // prefix_chunk
    suffix_chunks = window_rows // suffix_chunk
    key_place = window_start + jnp.arange(window_rows, dtype=jnp.int32)
    key_request = jnp.sum((key_place[:, None] >= request_end[None, :]).astype(jnp.int32), 1)
    key_request = jnp.where(key_place >= 0, key_request, -1)
    key_request = key_request.reshape(suffix_chunks, suffix_chunk)
    key_place = key_place.reshape(suffix_chunks, suffix_chunk)

    tile_tokens = min(TILE_TOKENS, token_rows)
    tile_count = token_rows // tile_tokens
    tile_rows = tile_tokens * repeat_count
    first_token = jnp.arange(tile_count, dtype=jnp.int32) * tile_tokens
    last_token = first_token + tile_tokens - 1
    p_lo = group_of[first_token]
    p_hi = group_of[last_token] + 1
    s_lo = jnp.maximum((starts[request[first_token]] - window_start) // suffix_chunk, 0)
    s_hi = jnp.minimum((position[last_token] - window_start) // suffix_chunk + 1, suffix_chunks)
    table = jnp.stack([p_lo, p_hi, s_lo, s_hi], 1).reshape(-1).astype(jnp.int32)

    query_rows = jnp.transpose(queries, (1, 0, 2, 3)).reshape(
        kv_heads, token_rows * repeat_count, HD
    )
    row_group = jnp.repeat(group_of, repeat_count)[:, None]
    row_request = jnp.repeat(request, repeat_count)[:, None]
    row_place = jnp.repeat(position, repeat_count)[:, None]

    def whole(shape):
        return pl.BlockSpec(shape, lambda tile, table: (0,) * len(shape))

    def half(shape, index):
        return pl.BlockSpec((kv_heads,) + shape[1:], lambda tile, table: (index, 0, 0))

    def prefix_half(index):
        shape = (G, kv_heads, HD, prefix_total)
        return pl.BlockSpec(shape, lambda tile, table: (0, index, 0, 0))

    row_spec = pl.BlockSpec((tile_rows, 1), lambda tile, table: (tile, 0))
    rows_total = token_rows * repeat_count
    state_shapes = [
        jax.ShapeDtypeStruct((kv_heads, rows_total, 1), jnp.float32),
        jax.ShapeDtypeStruct((kv_heads, rows_total, 1), jnp.float32),
        jax.ShapeDtypeStruct((kv_heads, rows_total, HD), jnp.float32),
    ]
    state_specs = [
        pl.BlockSpec((kv_heads, tile_rows, 1), lambda tile, table: (0, tile, 0)),
        pl.BlockSpec((kv_heads, tile_rows, 1), lambda tile, table: (0, tile, 0)),
        pl.BlockSpec((kv_heads, tile_rows, HD), lambda tile, table: (0, tile, 0)),
    ]
    query_spec = pl.BlockSpec((kv_heads, tile_rows, HD), lambda tile, table: (0, tile, 0))
    state = pl.pallas_call(
        functools.partial(suffix_kernel, kv_heads=kv_heads, suffix_chunk=suffix_chunk),
        grid_spec=pltpu.PrefetchScalarGridSpec(
            num_scalar_prefetch=1,
            grid=(tile_count,),
            in_specs=[
                query_spec,
                row_spec,
                row_spec,
                half(suffix_window.shape, 0),
                half(suffix_window.shape, 1),
                whole(key_request.shape),
                whole(key_place.shape),
            ],
            out_specs=state_specs,
        ),
        out_shape=state_shapes,
    )(table, query_rows, row_request, row_place, suffix_window, suffix_window, key_request, key_place)
    context = pl.pallas_call(
        functools.partial(
            prefix_kernel,
            kv_heads=kv_heads,
            prefix_chunk=prefix_chunk,
            parts_per_group=chunks_per_group,
        ),
        grid_spec=pltpu.PrefetchScalarGridSpec(
            num_scalar_prefetch=1,
            grid=(tile_count,),
            in_specs=[query_spec, row_spec, prefix_half(0), prefix_half(1)] + state_specs,
            out_specs=query_spec,
            scratch_shapes=[
                pltpu.VMEM((1, tile_rows, 1), jnp.float32),
                pltpu.VMEM((1, tile_rows, 1), jnp.float32),
                pltpu.VMEM((1, tile_rows, HD), jnp.float32),
            ],
        ),
        out_shape=jax.ShapeDtypeStruct((kv_heads, rows_total, HD), jnp.bfloat16),
    )(table, query_rows, row_group, all_prefix, all_prefix, *state)
    context = jnp.transpose(
        context.reshape(kv_heads, token_rows, repeat_count, HD), (1, 0, 2, 3)
    ).reshape(token_rows, query_heads * HD)
    mixture = jnp.dot(context, w_out, preferred_element_type=jnp.float32)
    mp_devices = lax.axis_size("mp")
    own_columns = lax.dynamic_slice_in_dim(activations, mp_index * part_width, part_width, 1)
    if mp_devices == 2:
        kept = lax.dynamic_slice_in_dim(mixture, mp_index * part_width, part_width, 1)
        sent = lax.dynamic_slice_in_dim(mixture, (1 - mp_index) * part_width, part_width, 1)
        received = lax.ppermute(sent.astype(jnp.bfloat16), "mp", [(0, 1), (1, 0)])
        hidden = (own_columns + (kept + received.astype(jnp.float32))).astype(jnp.bfloat16)
    else:
        mixture = lax.psum_scatter(
            mixture.astype(jnp.bfloat16), "mp", scatter_dimension=1, tiled=True
        ).astype(jnp.float32)
        hidden = (own_columns + mixture).astype(jnp.bfloat16)
    local_last = request_end - 1 - seq_index * token_rows
    onehot = (local_last[:, None] == jnp.arange(token_rows, dtype=jnp.int32)[None, :]).astype(
        jnp.bfloat16
    )
    last_part = jnp.dot(onehot, hidden, preferred_element_type=jnp.float32).astype(jnp.bfloat16)
    summed = butterfly(last_part, "seq", jnp.add)
    if summed is None:
        summed = lax.psum(last_part, "seq")
    last_rows = lax.all_gather(summed, "mp", axis=1, tiled=True).astype(jnp.float32)
    inv_rms = lax.rsqrt(jnp.mean(last_rows * last_rows, -1, keepdims=True) + epsilon)
    last_normed = (last_rows * final_gain.astype(jnp.float32) * inv_rms).astype(jnp.bfloat16)
    logits = jnp.dot(last_normed, w_head, preferred_element_type=jnp.float32)
    local_best = jnp.max(logits, -1)
    best_seq = butterfly(local_best, "seq", jnp.maximum)
    best_all = None if best_seq is None else butterfly(best_seq, "mp", jnp.maximum)
    greatest = lax.pmax(local_best, ("seq", "mp")) if best_all is None else best_all
    return (hidden, suffix_cache, last_normed, greatest)


def solution(mesh):
    return jax.shard_map(
        per_device,
        mesh=mesh,
        in_specs=(
            P("seq", None),
            P(),
            P(None, "seq", None),
            P(),
            P(None, "mp"),
            P(),
            P("mp", None),
            P(),
            P(None, ("seq", "mp")),
        ),
        out_specs=(P("seq", "mp"), P("seq", None), P(), P()),
        check_vma=False,
    )
```
